32 devices in a mesh: ens: 2 (over x), tile: 8 (over z, y), comp: 2 (over core).
Axes of the slice: x: 2, y: 2, z: 4, core: 2. Of those that a mesh axis runs over, the one named last changes fastest.
Arguments:
- increment: bfloat16 [64, 128, 256], P(('ens', 'tile'), None, 'comp'), parts along dimension 0, may hold values from -6 to 6
- land_sea: int32 [32, 128], P('tile'), may hold values 0 or 1
- kernel_x: float32 [41, 256], P(None, 'comp'), may hold values from -1 to 1
- kernel_y: float32 [41, 256], P(None, 'comp'), may hold values from -1 to 1
- balance: bfloat16 [8, 256, 256], P('tile', 'comp'), may hold values from -0.375 to 0.375
Outputs:
- filtered: bfloat16 [64, 128, 256], P('ens', 'tile', 'comp'), parts along dimension 0
The draws below stay inside these ranges and needn't reach their ends.
There are 2 independent parts, one for each index of `ens`. The reference program is written for one: setup_inputs(seed, part) draws one part's arguments, and reference() takes and returns one part's arrays. A program takes and returns all parts, laid end to end along the dimension named above; an argument that names none is the same for every part. Nothing has to cross between parts.
All inputs are finite; a program needn't handle non-finite values. No bound on the sum of `land_sea` on one device may be relied on, other than what follows from the above.
Results may differ from the reference program's by a relative error of at most 0.0057.
Values may be sent and summed in bfloat16 or wider, within the bound.
No kernel may reach another device: no remote copies, remote signals or barrier semaphores. Data moves between devices by JAX's collectives and lax.ppermute only.
A program may use at most 64 MiB of HBM per device.

```python
import jax
import jax.numpy as jnp
from jax import lax

C = 256
TAPS = 41
RY = 4
NY = 32
NX = 128
NS = 8


def place_ends(array, key, low, largest):
    extent = array.shape
    spot = [jax.random.randint(jax.random.fold_in(key, axis), (), 0, extent[axis]) for axis in range(len(extent))]
    array = array.at[tuple(spot)].set(low)
    longest = extent.index(max(extent))
    spot[longest] = (spot[longest] + 1) % extent[longest]
    return array.at[tuple(spot)].set(largest)


def block_levels(rng, extent, split, low, largest):
    factor_of = 1.0
    for position, blocks in split:
        heights = jax.random.uniform(jax.random.fold_in(jax.random.fold_in(rng, 6), position), (blocks,), jnp.float32, low / len(split), largest / len(split))
        factor_of = factor_of * jnp.repeat(jnp.exp(heights), extent[position] // blocks).reshape((-1,) + (1,) * (len(extent) - 1 - position))
    return factor_of


def gaussian(stream_key, extent, width, reach, pieces=(), kind=jnp.bfloat16):
    gain = block_levels(stream_key, extent, pieces, -0.22, 0.18) if pieces else 1.0
    drawn = jax.random.normal(stream_key, extent, jnp.float32) * width * gain
    return jnp.minimum(jnp.maximum(drawn, -reach), reach).astype(kind)


def setup_inputs(seed: int = 0, part: int = 0) -> dict:
    arg_keys = jax.random.split(jax.random.key(seed), 6)
    part_splits = jax.random.split(jax.random.fold_in(arg_keys[5], part), 6)
    increment = gaussian(part_splits[0], (NY, NX, C), 1.0, 6.0, ((0, 8), (2, 2)))
    land_sea = place_ends((jax.random.randint(arg_keys[1], (NY, NX), 0, 10) < 7).astype(jnp.int32), jax.random.fold_in(arg_keys[1], 1), 0, 1)
    kernel_x = gaussian(arg_keys[2], (TAPS, C), TAPS ** -0.5, 1.0, ((1, 2),), jnp.float32)
    kernel_y = gaussian(arg_keys[3], (TAPS, C), TAPS ** -0.5, 1.0, ((1, 2),), jnp.float32)
    balance = gaussian(arg_keys[4], (NS, C, C), C ** -0.5, 0.375, ((0, 8), (1, 2)))
    return {"increment": increment, "land_sea": land_sea, "kernel_x": kernel_x, "kernel_y": kernel_y, "balance": balance}


def reference(increment, land_sea, kernel_x, kernel_y, balance):
    sea = land_sea.astype(jnp.float32)[:, :, None]
    masked = increment.astype(jnp.float32) * sea
    half_taps = (TAPS - 1) // 2
    zonal = jnp.zeros(masked.shape, jnp.float32)
    for offset in range(TAPS):
        zonal = zonal + kernel_x[offset].astype(jnp.float32) * jnp.roll(masked, half_taps - offset, axis=1)
    zonal = (zonal * sea).astype(jnp.bfloat16)
    rows_all = zonal.shape[0]
    banded = zonal.reshape((NS, RY) + zonal.shape[1:])

    def apply_block(pair):
        return jnp.einsum("rxj,ij->rxi", pair[0].astype(jnp.float32), pair[1].astype(jnp.float32)).astype(jnp.bfloat16)

    mixed = lax.map(apply_block, (banded, balance)).reshape(zonal.shape)
    padded = jnp.pad(mixed.astype(jnp.float32), ((half_taps, half_taps), (0, 0), (0, 0)))
    filtered = jnp.zeros(mixed.shape, jnp.float32)
    for offset in range(TAPS):
        filtered = filtered + kernel_y[offset].astype(jnp.float32) * padded[offset:offset + rows_all]
    return filtered.astype(jnp.bfloat16)
```

```python
import functools

import jax
import jax.numpy as jnp
from jax import lax
from jax.experimental import pallas as pl
from jax.experimental.pallas import tpu as pltpu
from jax.sharding import PartitionSpec as P

F32 = jnp.float32
BF16 = jnp.bfloat16


def zonal_kernel(inc_ref, sea_ref, kx_ref, out_ref, ext_ref, seat_ref):
    rows, nx, ch = inc_ref.shape
    taps = kx_ref.shape[0]
    half = (taps - 1) // 2
    pad = ((half + 7) // 8) * 8
    span = nx + 2 * pad - 8
    sea = sea_ref[...].astype(F32)
    sea_pad = jnp.concatenate([sea, jnp.zeros((128 - rows, nx), F32)], axis=0)
    seat_ref[...] = jnp.transpose(sea_pad)
    chunk = min(nx, 64)
    for r in range(rows):
        col = seat_ref[:, r : r + 1]
        m = inc_ref[r].astype(F32) * col
        ext = jnp.concatenate([m[nx - pad :], m, m[:pad]], axis=0)
        for s in range(8):
            ext_ref[s] = ext[s : s + span]

        def body(i, carry, r=r):
            x0 = pl.multiple_of(i * chunk, chunk)
            acc = jnp.zeros((chunk, ch), F32)
            for k in range(taps):
                e = k - half + pad
                q, s = divmod(e, 8)
                acc = acc + kx_ref[k : k + 1, :] * ext_ref[s, pl.ds(x0 + 8 * q, chunk), :]
            mask = seat_ref[pl.ds(x0, chunk), r : r + 1]
            out_ref[r, pl.ds(x0, chunk), :] = (acc * mask).astype(out_ref.dtype)
            return carry

        n_chunks = nx // chunk
        lax.fori_loop(0, n_chunks, body, 0, unroll=n_chunks <= 4)


def zonal(inc, sea, kx):
    rows, nx, ch = inc.shape
    taps = kx.shape[0]
    pad = (((taps - 1) // 2 + 7) // 8) * 8
    return pl.pallas_call(
        zonal_kernel,
        out_shape=jax.ShapeDtypeStruct(inc.shape, BF16),
        scratch_shapes=[
            pltpu.VMEM((8, nx + 2 * pad - 8, ch), F32),
            pltpu.VMEM((nx, 128), F32),
        ],
        cost_estimate=pl.CostEstimate(
            flops=2 * taps * inc.size, transcendentals=0, bytes_accessed=4 * inc.size
        ),
    )(inc, sea, kx)


def balance_kernel(z_ref, b_ref, out_ref):
    nt, rows, width, _ = out_ref.shape
    b = b_ref[0]
    for r in range(rows):
        res = lax.dot_general(
            z_ref[r], b, (((1,), (1,)), ((), ())), preferred_element_type=F32
        ).astype(out_ref.dtype)
        for t in range(nt):
            out_ref[t, r] = res[t * width : (t + 1) * width]


def balance_mix(z, b, nt):
    rows, nx, cj = z.shape
    ci = b.shape[1]
    return pl.pallas_call(
        balance_kernel,
        out_shape=jax.ShapeDtypeStruct((nt, rows, nx // nt, ci), BF16),
        cost_estimate=pl.CostEstimate(
            flops=2 * rows * nx * cj * ci,
            transcendentals=0,
            bytes_accessed=2 * (z.size + b.size + rows * nx * ci),
        ),
    )(z, b)


def meridional_kernel(m_ref, ky_ref, out_ref, pad_ref):
    ny, w, ch = m_ref.shape
    taps = ky_ref.shape[0]
    half = (taps - 1) // 2
    pad_ref[0:half] = jnp.zeros((half, w, ch), F32)
    pad_ref[half + ny :] = jnp.zeros((half, w, ch), F32)
    pad_ref[half : half + ny] = m_ref[...].astype(F32)
    chunk = min(ny, 8)
    n_chunks = ny // chunk

    def rows_at(y0, lo, hi):
        acc = jnp.zeros((chunk, w, ch), F32)
        for k in range(lo, hi):
            acc = acc + ky_ref[k : k + 1, :][None] * pad_ref[pl.ds(y0 + k, chunk)]
        out_ref[pl.ds(y0, chunk)] = acc.astype(out_ref.dtype)

    if n_chunks <= 8:
        for c in range(n_chunks):
            y0 = c * chunk
            lo = max(0, half - y0 - chunk + 1)
            hi = min(taps, half + ny - y0)
            rows_at(y0, lo, hi)
    else:

        def body(i, carry):
            rows_at(pl.multiple_of(i * chunk, chunk), 0, taps)
            return carry

        lax.fori_loop(0, n_chunks, body, 0)


def meridional(m, ky):
    ny, w, ch = m.shape
    taps = ky.shape[0]
    half = (taps - 1) // 2
    return pl.pallas_call(
        meridional_kernel,
        out_shape=jax.ShapeDtypeStruct(m.shape, BF16),
        scratch_shapes=[pltpu.VMEM((ny + 2 * half, w, ch), F32)],
        cost_estimate=pl.CostEstimate(
            flops=2 * taps * m.size, transcendentals=0, bytes_accessed=4 * m.size
        ),
    )(m, ky)


def per_device(nt, increment, land_sea, kernel_x, kernel_y, balance):
    z = zonal(increment, land_sea, kernel_x)
    z_all = lax.all_gather(z, "comp", axis=2, tiled=True)
    mixed = balance_mix(z_all, balance, nt)
    moved = lax.all_to_all(mixed, "tile", split_axis=0, concat_axis=0, tiled=True)
    nt_, rows, width, ch = moved.shape
    return meridional(moved.reshape(nt_ * rows, width, ch), kernel_y)


def solution(mesh):
    nt = mesh.shape["tile"]
    return jax.shard_map(
        functools.partial(per_device, nt),
        mesh=mesh,
        in_specs=(
            P(("ens", "tile"), None, "comp"),
            P("tile", None),
            P(None, "comp"),
            P(None, "comp"),
            P("tile", "comp", None),
        ),
        out_specs=P("ens", "tile", "comp"),
        check_vma=False,
    )
```

```python
import functools

import jax
import jax.numpy as jnp
from jax import lax
from jax.experimental import pallas as pl
from jax.experimental.pallas import tpu as pltpu
from jax.sharding import PartitionSpec as P

F32 = jnp.float32
VMEM_SPEC = pl.BlockSpec(memory_space=pltpu.VMEM)
SMALL_VMEM = pltpu.CompilerParams(vmem_limit_bytes=8 * 1024 * 1024)
BF16 = jnp.bfloat16


def zonal_kernel(inc_ref, sea_ref, kx_ref, out_ref, ext_ref, seat_ref):
    rows, nx, ch = inc_ref.shape
    taps = kx_ref.shape[0]
    half = (taps - 1) // 2
    pad = ((half + 7) // 8) * 8
    span = nx + 2 * pad - 8
    sea = sea_ref[...].astype(F32)
    sea_pad = jnp.concatenate([sea, jnp.zeros((128 - rows, nx), F32)], axis=0)
    seat_ref[...] = jnp.transpose(sea_pad)
    chunk = min(nx, 64)
    for r in range(rows):
        col = seat_ref[:, r : r + 1]
        m = inc_ref[r].astype(F32) * col
        ext = jnp.concatenate([m[nx - pad :], m, m[:pad]], axis=0)
        for s in range(8):
            ext_ref[s] = ext[s : s + span]

        def body(i, carry, r=r):
            x0 = pl.multiple_of(i * chunk, chunk)
            acc = jnp.zeros((chunk, ch), F32)
            for k in range(taps):
                e = k - half + pad
                q, s = divmod(e, 8)
                acc = acc + kx_ref[k : k + 1, :] * ext_ref[s, pl.ds(x0 + 8 * q, chunk), :]
            mask = seat_ref[pl.ds(x0, chunk), r : r + 1]
            out_ref[r, pl.ds(x0, chunk), :] = (acc * mask).astype(out_ref.dtype)
            return carry

        n_chunks = nx // chunk
        lax.fori_loop(0, n_chunks, body, 0, unroll=n_chunks <= 4)


def zonal(inc, sea, kx):
    rows, nx, ch = inc.shape
    taps = kx.shape[0]
    pad = (((taps - 1) // 2 + 7) // 8) * 8
    return pl.pallas_call(
        zonal_kernel,
        out_shape=jax.ShapeDtypeStruct(inc.shape, BF16),
        in_specs=[VMEM_SPEC] * 3,
        out_specs=VMEM_SPEC,
        scratch_shapes=[
            pltpu.VMEM((8, nx + 2 * pad - 8, ch), F32),
            pltpu.VMEM((nx, 128), F32),
        ],
        compiler_params=SMALL_VMEM,
        cost_estimate=pl.CostEstimate(
            flops=2 * taps * inc.size, transcendentals=0, bytes_accessed=4 * inc.size
        ),
    )(inc, sea, kx)


def balance_kernel(z_ref, b_ref, out_ref):
    nt, rows, width, _ = out_ref.shape
    b = b_ref[0]
    for r in range(rows):
        res = lax.dot_general(
            z_ref[r], b, (((1,), (1,)), ((), ())), preferred_element_type=F32
        ).astype(out_ref.dtype)
        for t in range(nt):
            out_ref[t, r] = res[t * width : (t + 1) * width]


def balance_mix(z, b, nt):
    rows, nx, cj = z.shape
    ci = b.shape[1]
    return pl.pallas_call(
        balance_kernel,
        out_shape=jax.ShapeDtypeStruct((nt, rows, nx // nt, ci), BF16),
        in_specs=[VMEM_SPEC] * 2,
        out_specs=VMEM_SPEC,
        compiler_params=SMALL_VMEM,
        cost_estimate=pl.CostEstimate(
            flops=2 * rows * nx * cj * ci,
            transcendentals=0,
            bytes_accessed=2 * (z.size + b.size + rows * nx * ci),
        ),
    )(z, b)


def meridional_kernel(m_ref, ky_ref, out_ref, pad_ref):
    ny, w, ch = m_ref.shape
    taps = ky_ref.shape[0]
    half = (taps - 1) // 2
    pad_ref[0:half] = jnp.zeros((half, w, ch), F32)
    pad_ref[half + ny :] = jnp.zeros((half, w, ch), F32)
    pad_ref[half : half + ny] = m_ref[...].astype(F32)
    chunk = min(ny, 8)
    n_chunks = ny // chunk

    def rows_at(y0, lo, hi):
        acc = jnp.zeros((chunk, w, ch), F32)
        for k in range(lo, hi):
            acc = acc + ky_ref[k : k + 1, :][None] * pad_ref[pl.ds(y0 + k, chunk)]
        out_ref[pl.ds(y0, chunk)] = acc.astype(out_ref.dtype)

    if n_chunks <= 8:
        for c in range(n_chunks):
            y0 = c * chunk
            lo = max(0, half - y0 - chunk + 1)
            hi = min(taps, half + ny - y0)
            rows_at(y0, lo, hi)
    else:

        def body(i, carry):
            rows_at(pl.multiple_of(i * chunk, chunk), 0, taps)
            return carry

        lax.fori_loop(0, n_chunks, body, 0)


def meridional(m, ky):
    ny, w, ch = m.shape
    taps = ky.shape[0]
    half = (taps - 1) // 2
    return pl.pallas_call(
        meridional_kernel,
        out_shape=jax.ShapeDtypeStruct(m.shape, BF16),
        in_specs=[VMEM_SPEC] * 2,
        out_specs=VMEM_SPEC,
        scratch_shapes=[pltpu.VMEM((ny + 2 * half, w, ch), F32)],
        compiler_params=SMALL_VMEM,
        cost_estimate=pl.CostEstimate(
            flops=2 * taps * m.size, transcendentals=0, bytes_accessed=4 * m.size
        ),
    )(m, ky)


def per_device(nt, increment, land_sea, kernel_x, kernel_y, balance):
    z = zonal(increment, land_sea, kernel_x)
    z_all = lax.all_gather(z, "comp", axis=2, tiled=True)
    mixed = balance_mix(z_all, balance, nt)
    moved = lax.all_to_all(mixed, "tile", split_axis=0, concat_axis=0, tiled=True)
    nt_, rows, width, ch = moved.shape
    return meridional(moved.reshape(nt_ * rows, width, ch), kernel_y)


def solution(mesh):
    nt = mesh.shape["tile"]
    return jax.shard_map(
        functools.partial(per_device, nt),
        mesh=mesh,
        in_specs=(
            P(("ens", "tile"), None, "comp"),
            P("tile", None),
            P(None, "comp"),
            P(None, "comp"),
            P("tile", "comp", None),
        ),
        out_specs=P("ens", "tile", "comp"),
        check_vma=False,
    )
```

```python
import functools

import jax
import jax.numpy as jnp
from jax import lax
from jax.experimental import pallas as pl
from jax.experimental.pallas import tpu as pltpu
from jax.sharding import PartitionSpec as P

F32 = jnp.float32
VMEM_SPEC = pl.BlockSpec(memory_space=pltpu.VMEM)
SMALL_VMEM = pltpu.CompilerParams(vmem_limit_bytes=8 * 1024 * 1024)
BF16 = jnp.bfloat16


def zonal_kernel(inc_hbm, sea_hbm, kx_hbm, out_ref, inc_ref, sea_ref, kx_ref, ext_ref, seat_ref, sems):
    rows, nx, ch = inc_ref.shape
    taps = kx_ref.shape[0]
    half = (taps - 1) // 2
    pad = ((half + 7) // 8) * 8
    span = nx + 2 * pad - 8
    copies = [
        pltpu.make_async_copy(sea_hbm, sea_ref, sems.at[rows]),
        pltpu.make_async_copy(kx_hbm, kx_ref, sems.at[rows + 1]),
    ]
    rows_in = [pltpu.make_async_copy(inc_hbm.at[r], inc_ref.at[r], sems.at[r]) for r in range(rows)]
    for c in copies + rows_in:
        c.start()
    for c in copies:
        c.wait()
    sea = sea_ref[...].astype(F32)
    sea_pad = jnp.concatenate([sea, jnp.zeros((128 - rows, nx), F32)], axis=0)
    seat_ref[...] = jnp.transpose(sea_pad)
    chunk = min(nx, 64)
    for r in range(rows):
        rows_in[r].wait()
        col = seat_ref[:, r : r + 1]
        m = inc_ref[r].astype(F32) * col
        ext = jnp.concatenate([m[nx - pad :], m, m[:pad]], axis=0)
        for s in range(8):
            ext_ref[s] = ext[s : s + span]

        def body(i, carry, r=r):
            x0 = pl.multiple_of(i * chunk, chunk)
            acc = jnp.zeros((chunk, ch), F32)
            for k in range(taps):
                e = k - half + pad
                q, s = divmod(e, 8)
                acc = acc + kx_ref[k : k + 1, :] * ext_ref[s, pl.ds(x0 + 8 * q, chunk), :]
            mask = seat_ref[pl.ds(x0, chunk), r : r + 1]
            out_ref[r, pl.ds(x0, chunk), :] = (acc * mask).astype(out_ref.dtype)
            return carry

        n_chunks = nx // chunk
        lax.fori_loop(0, n_chunks, body, 0, unroll=n_chunks <= 4)


def zonal(inc, sea, kx):
    rows, nx, ch = inc.shape
    taps = kx.shape[0]
    pad = (((taps - 1) // 2 + 7) // 8) * 8
    any_spec = pl.BlockSpec(memory_space=pltpu.HBM)
    return pl.pallas_call(
        zonal_kernel,
        out_shape=jax.ShapeDtypeStruct(inc.shape, BF16),
        in_specs=[any_spec] * 3,
        out_specs=VMEM_SPEC,
        scratch_shapes=[
            pltpu.VMEM(inc.shape, BF16),
            pltpu.VMEM(sea.shape, sea.dtype),
            pltpu.VMEM(kx.shape, F32),
            pltpu.VMEM((8, nx + 2 * pad - 8, ch), F32),
            pltpu.VMEM((nx, 128), F32),
            pltpu.SemaphoreType.DMA((rows + 2,)),
        ],
        cost_estimate=pl.CostEstimate(
            flops=2 * taps * inc.size, transcendentals=0, bytes_accessed=4 * inc.size
        ),
    )(inc, sea, kx)


def balance_kernel(z_ref, b_ref, out_ref):
    nt, rows, width, _ = out_ref.shape
    b = b_ref[0]
    for r in range(rows):
        res = lax.dot_general(
            z_ref[r], b, (((1,), (1,)), ((), ())), preferred_element_type=F32
        ).astype(out_ref.dtype)
        for t in range(nt):
            out_ref[t, r] = res[t * width : (t + 1) * width]


def balance_mix(z, b, nt):
    rows, nx, cj = z.shape
    ci = b.shape[1]
    return pl.pallas_call(
        balance_kernel,
        out_shape=jax.ShapeDtypeStruct((nt, rows, nx // nt, ci), BF16),
        in_specs=[VMEM_SPEC] * 2,
        out_specs=VMEM_SPEC,
        compiler_params=SMALL_VMEM,
        cost_estimate=pl.CostEstimate(
            flops=2 * rows * nx * cj * ci,
            transcendentals=0,
            bytes_accessed=2 * (z.size + b.size + rows * nx * ci),
        ),
    )(z, b)


def meridional_kernel(m_ref, ky_ref, out_ref, pad_ref):
    ny, w, ch = m_ref.shape
    taps = ky_ref.shape[0]
    half = (taps - 1) // 2
    pad_ref[0:half] = jnp.zeros((half, w, ch), F32)
    pad_ref[half + ny :] = jnp.zeros((half, w, ch), F32)
    pad_ref[half : half + ny] = m_ref[...].astype(F32)
    chunk = min(ny, 8)
    n_chunks = ny // chunk

    def rows_at(y0, lo, hi):
        acc = jnp.zeros((chunk, w, ch), F32)
        for k in range(lo, hi):
            acc = acc + ky_ref[k : k + 1, :][None] * pad_ref[pl.ds(y0 + k, chunk)]
        out_ref[pl.ds(y0, chunk)] = acc.astype(out_ref.dtype)

    if n_chunks <= 8:
        for c in range(n_chunks):
            y0 = c * chunk
            lo = max(0, half - y0 - chunk + 1)
            hi = min(taps, half + ny - y0)
            rows_at(y0, lo, hi)
    else:

        def body(i, carry):
            rows_at(pl.multiple_of(i * chunk, chunk), 0, taps)
            return carry

        lax.fori_loop(0, n_chunks, body, 0)


def meridional(m, ky):
    ny, w, ch = m.shape
    taps = ky.shape[0]
    half = (taps - 1) // 2
    return pl.pallas_call(
        meridional_kernel,
        out_shape=jax.ShapeDtypeStruct(m.shape, BF16),
        in_specs=[VMEM_SPEC] * 2,
        out_specs=VMEM_SPEC,
        scratch_shapes=[pltpu.VMEM((ny + 2 * half, w, ch), F32)],
        compiler_params=SMALL_VMEM,
        cost_estimate=pl.CostEstimate(
            flops=2 * taps * m.size, transcendentals=0, bytes_accessed=4 * m.size
        ),
    )(m, ky)


def per_device(nt, increment, land_sea, kernel_x, kernel_y, balance):
    z = zonal(increment, land_sea, kernel_x)
    z_all = lax.all_gather(z, "comp", axis=2, tiled=True)
    mixed = balance_mix(z_all, balance, nt)
    moved = lax.all_to_all(mixed, "tile", split_axis=0, concat_axis=0, tiled=True)
    nt_, rows, width, ch = moved.shape
    return meridional(moved.reshape(nt_ * rows, width, ch), kernel_y)


def solution(mesh):
    nt = mesh.shape["tile"]
    return jax.shard_map(
        functools.partial(per_device, nt),
        mesh=mesh,
        in_specs=(
            P(("ens", "tile"), None, "comp"),
            P("tile", None),
            P(None, "comp"),
            P(None, "comp"),
            P("tile", "comp", None),
        ),
        out_specs=P("ens", "tile", "comp"),
        check_vma=False,
    )
```

```python
import functools

import jax
import jax.numpy as jnp
from jax import lax
from jax.experimental import pallas as pl
from jax.experimental.pallas import tpu as pltpu
from jax.sharding import PartitionSpec as P

F32 = jnp.float32
VMEM_SPEC = pl.BlockSpec(memory_space=pltpu.VMEM)
SMALL_VMEM = pltpu.CompilerParams(vmem_limit_bytes=8 * 1024 * 1024)
BF16 = jnp.bfloat16


def zonal_kernel(inc_hbm, sea_hbm, kx_hbm, out_ref, inc_ref, sea_ref, kx_ref, ext_ref, seat_ref, sems):
    rows, nx, ch = inc_ref.shape
    taps = kx_ref.shape[0]
    half = (taps - 1) // 2
    pad = ((half + 7) // 8) * 8
    span = nx + 2 * pad - 8
    copies = [
        pltpu.make_async_copy(sea_hbm, sea_ref, sems.at[rows]),
        pltpu.make_async_copy(kx_hbm, kx_ref, sems.at[rows + 1]),
    ]
    rows_in = [pltpu.make_async_copy(inc_hbm.at[r], inc_ref.at[r], sems.at[r]) for r in range(rows)]
    for c in copies + rows_in:
        c.start()
    for c in copies:
        c.wait()
    sea = sea_ref[...].astype(F32)
    sea_pad = jnp.concatenate([sea, jnp.zeros((128 - rows, nx), F32)], axis=0)
    seat_ref[...] = jnp.transpose(sea_pad)
    chunk = min(nx, 64)
    for r in range(rows):
        rows_in[r].wait()
        col = seat_ref[:, r : r + 1]
        m = inc_ref[r].astype(F32) * col
        ext = jnp.concatenate([m[nx - pad :], m, m[:pad]], axis=0)
        for s in range(8):
            ext_ref[s] = ext[s : s + span]

        def body(i, carry, r=r):
            x0 = pl.multiple_of(i * chunk, chunk)
            acc = jnp.zeros((chunk, ch), F32)
            for k in range(taps):
                e = k - half + pad
                q, s = divmod(e, 8)
                acc = acc + kx_ref[k : k + 1, :] * ext_ref[s, pl.ds(x0 + 8 * q, chunk), :]
            mask = seat_ref[pl.ds(x0, chunk), r : r + 1]
            out_ref[r, pl.ds(x0, chunk), :] = (acc * mask).astype(out_ref.dtype)
            return carry

        n_chunks = nx // chunk
        lax.fori_loop(0, n_chunks, body, 0, unroll=n_chunks <= 4)


def zonal(inc, sea, kx):
    rows, nx, ch = inc.shape
    taps = kx.shape[0]
    pad = (((taps - 1) // 2 + 7) // 8) * 8
    any_spec = pl.BlockSpec(memory_space=pltpu.HBM)
    return pl.pallas_call(
        zonal_kernel,
        out_shape=jax.ShapeDtypeStruct(inc.shape, BF16),
        in_specs=[any_spec] * 3,
        out_specs=VMEM_SPEC,
        scratch_shapes=[
            pltpu.VMEM(inc.shape, BF16),
            pltpu.VMEM(sea.shape, sea.dtype),
            pltpu.VMEM(kx.shape, F32),
            pltpu.VMEM((8, nx + 2 * pad - 8, ch), F32),
            pltpu.VMEM((nx, 128), F32),
            pltpu.SemaphoreType.DMA((rows + 2,)),
        ],
        cost_estimate=pl.CostEstimate(
            flops=2 * taps * inc.size, transcendentals=0, bytes_accessed=4 * inc.size
        ),
    )(inc, sea, kx)


def balance_kernel(c_ref, z_ref, zo_ref, b_ref, out_ref):
    nt, rows, width, _ = out_ref.shape
    ch = z_ref.shape[2]
    c = c_ref[0]
    own = b_ref[0, :, pl.ds(pl.multiple_of(c * ch, ch), ch)]
    other = b_ref[0, :, pl.ds(pl.multiple_of((1 - c) * ch, ch), ch)]
    dims = (((1,), (1,)), ((), ()))
    for r in range(rows):
        res = lax.dot_general(z_ref[r], own, dims, preferred_element_type=F32)
        res = res + lax.dot_general(zo_ref[r], other, dims, preferred_element_type=F32)
        res = res.astype(out_ref.dtype)
        for t in range(nt):
            out_ref[t, r] = res[t * width : (t + 1) * width]


def balance_mix(c, z, zo, b, nt):
    rows, nx, ch = z.shape
    ci = b.shape[1]
    return pl.pallas_call(
        balance_kernel,
        out_shape=jax.ShapeDtypeStruct((nt, rows, nx // nt, ci), BF16),
        in_specs=[pl.BlockSpec(memory_space=pltpu.SMEM)] + [VMEM_SPEC] * 3,
        out_specs=VMEM_SPEC,
        compiler_params=SMALL_VMEM,
        cost_estimate=pl.CostEstimate(
            flops=4 * rows * nx * ch * ci,
            transcendentals=0,
            bytes_accessed=2 * (2 * z.size + b.size + rows * nx * ci),
        ),
    )(c, z, zo, b)


def meridional_kernel(m_ref, ky_ref, out_ref, pad_ref):
    ny, w, ch = m_ref.shape
    taps = ky_ref.shape[0]
    half = (taps - 1) // 2
    pad_ref[0:half] = jnp.zeros((half, w, ch), F32)
    pad_ref[half + ny :] = jnp.zeros((half, w, ch), F32)
    pad_ref[half : half + ny] = m_ref[...].astype(F32)
    chunk = min(ny, 8)
    n_chunks = ny // chunk

    def rows_at(y0, lo, hi):
        acc = jnp.zeros((chunk, w, ch), F32)
        for k in range(lo, hi):
            acc = acc + ky_ref[k : k + 1, :][None] * pad_ref[pl.ds(y0 + k, chunk)]
        out_ref[pl.ds(y0, chunk)] = acc.astype(out_ref.dtype)

    if n_chunks <= 8:
        for c in range(n_chunks):
            y0 = c * chunk
            lo = max(0, half - y0 - chunk + 1)
            hi = min(taps, half + ny - y0)
            rows_at(y0, lo, hi)
    else:

        def body(i, carry):
            rows_at(pl.multiple_of(i * chunk, chunk), 0, taps)
            return carry

        lax.fori_loop(0, n_chunks, body, 0)


def meridional(m, ky):
    ny, w, ch = m.shape
    taps = ky.shape[0]
    half = (taps - 1) // 2
    return pl.pallas_call(
        meridional_kernel,
        out_shape=jax.ShapeDtypeStruct(m.shape, BF16),
        in_specs=[VMEM_SPEC] * 2,
        out_specs=VMEM_SPEC,
        scratch_shapes=[pltpu.VMEM((ny + 2 * half, w, ch), F32)],
        compiler_params=SMALL_VMEM,
        cost_estimate=pl.CostEstimate(
            flops=2 * taps * m.size, transcendentals=0, bytes_accessed=4 * m.size
        ),
    )(m, ky)


def per_device(nt, increment, land_sea, kernel_x, kernel_y, balance):
    z = zonal(increment, land_sea, kernel_x)
    z_other = lax.ppermute(z, "comp", [(0, 1), (1, 0)])
    c = lax.axis_index("comp").astype(jnp.int32).reshape(1)
    mixed = balance_mix(c, z, z_other, balance, nt)
    moved = lax.all_to_all(mixed, "tile", split_axis=0, concat_axis=0, tiled=True)
    nt_, rows, width, ch = moved.shape
    return meridional(moved.reshape(nt_ * rows, width, ch), kernel_y)


def solution(mesh):
    nt = mesh.shape["tile"]
    return jax.shard_map(
        functools.partial(per_device, nt),
        mesh=mesh,
        in_specs=(
            P(("ens", "tile"), None, "comp"),
            P("tile", None),
            P(None, "comp"),
            P(None, "comp"),
            P("tile", "comp", None),
        ),
        out_specs=P("ens", "tile", "comp"),
        check_vma=False,
    )
```

```python
import functools

import jax
import jax.numpy as jnp
from jax import lax
from jax.experimental import pallas as pl
from jax.experimental.pallas import tpu as pltpu
from jax.sharding import PartitionSpec as P

F32 = jnp.float32
VMEM_SPEC = pl.BlockSpec(memory_space=pltpu.VMEM)
SMALL_VMEM = pltpu.CompilerParams(vmem_limit_bytes=8 * 1024 * 1024)
BF16 = jnp.bfloat16


def zonal_kernel(inc_ref, sea_ref, kx_ref, out_ref, ext_ref, seat_ref):
    rows, nx, ch = inc_ref.shape
    taps = kx_ref.shape[0]
    half = (taps - 1) // 2
    pad = ((half + 7) // 8) * 8
    span = nx + 2 * pad - 8
    sea = sea_ref[...].astype(F32)
    sea_pad = jnp.concatenate([sea, jnp.zeros((128 - rows, nx), F32)], axis=0)
    seat_ref[...] = jnp.transpose(sea_pad)
    chunk = min(nx, 64)
    for r in range(rows):
        col = seat_ref[:, r : r + 1]
        m = inc_ref[r].astype(F32) * col
        ext = jnp.concatenate([m[nx - pad :], m, m[:pad]], axis=0)
        for s in range(8):
            ext_ref[s] = ext[s : s + span]

        def body(i, carry, r=r):
            x0 = pl.multiple_of(i * chunk, chunk)
            acc = jnp.zeros((chunk, ch), F32)
            for k in range(taps):
                e = k - half + pad
                q, s = divmod(e, 8)
                acc = acc + kx_ref[k : k + 1, :] * ext_ref[s, pl.ds(x0 + 8 * q, chunk), :]
            mask = seat_ref[pl.ds(x0, chunk), r : r + 1]
            out_ref[r, pl.ds(x0, chunk), :] = (acc * mask).astype(out_ref.dtype)
            return carry

        n_chunks = nx // chunk
        lax.fori_loop(0, n_chunks, body, 0, unroll=n_chunks <= 4)


def zonal(inc, sea, kx):
    rows, nx, ch = inc.shape
    taps = kx.shape[0]
    pad = (((taps - 1) // 2 + 7) // 8) * 8
    return pl.pallas_call(
        zonal_kernel,
        out_shape=jax.ShapeDtypeStruct(inc.shape, BF16),
        in_specs=[VMEM_SPEC] * 3,
        out_specs=VMEM_SPEC,
        scratch_shapes=[
            pltpu.VMEM((8, nx + 2 * pad - 8, ch), F32),
            pltpu.VMEM((nx, 128), F32),
        ],
        compiler_params=SMALL_VMEM,
        cost_estimate=pl.CostEstimate(
            flops=2 * taps * inc.size, transcendentals=0, bytes_accessed=4 * inc.size
        ),
    )(inc, sea, kx)


def balance_kernel(c_ref, z_ref, zo_ref, b_ref, out_ref):
    nt, rows, width, _ = out_ref.shape
    ch = z_ref.shape[2]
    c = c_ref[0]
    own = b_ref[0, :, pl.ds(pl.multiple_of(c * ch, ch), ch)]
    other = b_ref[0, :, pl.ds(pl.multiple_of((1 - c) * ch, ch), ch)]
    dims = (((1,), (1,)), ((), ()))
    for r in range(rows):
        res = lax.dot_general(z_ref[r], own, dims, preferred_element_type=F32)
        res = res + lax.dot_general(zo_ref[r], other, dims, preferred_element_type=F32)
        res = res.astype(out_ref.dtype)
        for t in range(nt):
            out_ref[t, r] = res[t * width : (t + 1) * width]


def balance_mix(c, z, zo, b, nt):
    rows, nx, ch = z.shape
    ci = b.shape[1]
    return pl.pallas_call(
        balance_kernel,
        out_shape=jax.ShapeDtypeStruct((nt, rows, nx // nt, ci), BF16),
        in_specs=[pl.BlockSpec(memory_space=pltpu.SMEM)] + [VMEM_SPEC] * 3,
        out_specs=VMEM_SPEC,
        compiler_params=SMALL_VMEM,
        cost_estimate=pl.CostEstimate(
            flops=4 * rows * nx * ch * ci,
            transcendentals=0,
            bytes_accessed=2 * (2 * z.size + b.size + rows * nx * ci),
        ),
    )(c, z, zo, b)


def meridional_kernel(m_ref, ky_ref, out_ref, pad_ref):
    ny, w, ch = m_ref.shape
    taps = ky_ref.shape[0]
    half = (taps - 1) // 2
    pad_ref[0:half] = jnp.zeros((half, w, ch), F32)
    pad_ref[half + ny :] = jnp.zeros((half, w, ch), F32)
    pad_ref[half : half + ny] = m_ref[...].astype(F32)
    chunk = min(ny, 8)
    n_chunks = ny // chunk

    def rows_at(y0, lo, hi):
        acc = jnp.zeros((chunk, w, ch), F32)
        for k in range(lo, hi):
            acc = acc + ky_ref[k : k + 1, :][None] * pad_ref[pl.ds(y0 + k, chunk)]
        out_ref[pl.ds(y0, chunk)] = acc.astype(out_ref.dtype)

    if n_chunks <= 8:
        for c in range(n_chunks):
            y0 = c * chunk
            lo = max(0, half - y0 - chunk + 1)
            hi = min(taps, half + ny - y0)
            rows_at(y0, lo, hi)
    else:

        def body(i, carry):
            rows_at(pl.multiple_of(i * chunk, chunk), 0, taps)
            return carry

        lax.fori_loop(0, n_chunks, body, 0)


def meridional(m, ky):
    ny, w, ch = m.shape
    taps = ky.shape[0]
    half = (taps - 1) // 2
    return pl.pallas_call(
        meridional_kernel,
        out_shape=jax.ShapeDtypeStruct(m.shape, BF16),
        in_specs=[VMEM_SPEC] * 2,
        out_specs=VMEM_SPEC,
        scratch_shapes=[pltpu.VMEM((ny + 2 * half, w, ch), F32)],
        compiler_params=SMALL_VMEM,
        cost_estimate=pl.CostEstimate(
            flops=2 * taps * m.size, transcendentals=0, bytes_accessed=4 * m.size
        ),
    )(m, ky)


def per_device(nt, increment, land_sea, kernel_x, kernel_y, balance):
    z = zonal(increment, land_sea, kernel_x)
    z_other = lax.ppermute(z, "comp", [(0, 1), (1, 0)])
    c = lax.axis_index("comp").astype(jnp.int32).reshape(1)
    mixed = balance_mix(c, z, z_other, balance, nt)
    moved = lax.all_to_all(mixed, "tile", split_axis=0, concat_axis=0, tiled=True)
    nt_, rows, width, ch = moved.shape
    return meridional(moved.reshape(nt_ * rows, width, ch), kernel_y)


def solution(mesh):
    nt = mesh.shape["tile"]
    return jax.shard_map(
        functools.partial(per_device, nt),
        mesh=mesh,
        in_specs=(
            P(("ens", "tile"), None, "comp"),
            P("tile", None),
            P(None, "comp"),
            P(None, "comp"),
            P("tile", "comp", None),
        ),
        out_specs=P("ens", "tile", "comp"),
        check_vma=False,
    )
```

```python
import functools

import jax
import jax.numpy as jnp
from jax import lax
from jax.experimental import pallas as pl
from jax.experimental.pallas import tpu as pltpu
from jax.sharding import PartitionSpec as P

F32 = jnp.float32
VMEM_SPEC = pl.BlockSpec(memory_space=pltpu.VMEM)
SMALL_VMEM = pltpu.CompilerParams(vmem_limit_bytes=8 * 1024 * 1024)
BF16 = jnp.bfloat16


def zonal_kernel(m_ref, kx_ref, out_ref, ext_ref):
    rows, nx, ch = m_ref.shape
    taps = kx_ref.shape[0]
    half = (taps - 1) // 2
    pad = ((half + 7) // 8) * 8
    span = nx + 2 * pad - 8
    chunk = min(nx, 64)
    for r in range(rows):
        m = m_ref[r].astype(F32)
        ext = jnp.concatenate([m[nx - pad :], m, m[:pad]], axis=0)
        for s in range(8):
            ext_ref[s] = ext[s : s + span]

        def body(i, carry, r=r):
            x0 = pl.multiple_of(i * chunk, chunk)
            acc = jnp.zeros((chunk, ch), F32)
            for k in range(taps):
                e = k - half + pad
                q, s = divmod(e, 8)
                acc = acc + kx_ref[k : k + 1, :] * ext_ref[s, pl.ds(x0 + 8 * q, chunk), :]
            out_ref[r, pl.ds(x0, chunk), :] = acc.astype(out_ref.dtype)
            return carry

        n_chunks = nx // chunk
        lax.fori_loop(0, n_chunks, body, 0, unroll=n_chunks <= 4)


def zonal(m, kx):
    rows, nx, ch = m.shape
    taps = kx.shape[0]
    pad = (((taps - 1) // 2 + 7) // 8) * 8
    return pl.pallas_call(
        zonal_kernel,
        out_shape=jax.ShapeDtypeStruct(m.shape, BF16),
        in_specs=[VMEM_SPEC] * 2,
        out_specs=VMEM_SPEC,
        scratch_shapes=[pltpu.VMEM((8, nx + 2 * pad - 8, ch), F32)],
        compiler_params=SMALL_VMEM,
        cost_estimate=pl.CostEstimate(
            flops=2 * taps * m.size, transcendentals=0, bytes_accessed=4 * m.size
        ),
    )(m, kx)


def balance_kernel(c_ref, z_ref, zo_ref, b_ref, sea_ref, out_ref, seat_ref):
    nt, rows, width, _ = out_ref.shape
    nx, ch = z_ref.shape[1], z_ref.shape[2]
    sea = sea_ref[...].astype(F32)
    sea_pad = jnp.concatenate([sea, jnp.zeros((128 - rows, nx), F32)], axis=0)
    seat_ref[...] = jnp.transpose(sea_pad)
    c = c_ref[0]
    own = b_ref[0, :, pl.ds(pl.multiple_of(c * ch, ch), ch)]
    other = b_ref[0, :, pl.ds(pl.multiple_of((1 - c) * ch, ch), ch)]
    dims = (((1,), (1,)), ((), ()))
    for r in range(rows):
        res = lax.dot_general(z_ref[r], own, dims, preferred_element_type=F32)
        res = res + lax.dot_general(zo_ref[r], other, dims, preferred_element_type=F32)
        res = (res * seat_ref[:, r : r + 1]).astype(out_ref.dtype)
        for t in range(nt):
            out_ref[t, r] = res[t * width : (t + 1) * width]


def balance_mix(c, z, zo, b, sea, nt):
    rows, nx, ch = z.shape
    ci = b.shape[1]
    return pl.pallas_call(
        balance_kernel,
        out_shape=jax.ShapeDtypeStruct((nt, rows, nx // nt, ci), BF16),
        in_specs=[pl.BlockSpec(memory_space=pltpu.SMEM)] + [VMEM_SPEC] * 4,
        out_specs=VMEM_SPEC,
        scratch_shapes=[pltpu.VMEM((nx, 128), F32)],
        compiler_params=SMALL_VMEM,
        cost_estimate=pl.CostEstimate(
            flops=4 * rows * nx * ch * ci,
            transcendentals=0,
            bytes_accessed=2 * (2 * z.size + b.size + rows * nx * ci),
        ),
    )(c, z, zo, b, sea)


def meridional_kernel(m_ref, ky_ref, out_ref, pad_ref):
    ny, w, ch = m_ref.shape
    taps = ky_ref.shape[0]
    half = (taps - 1) // 2
    pad_ref[0:half] = jnp.zeros((half, w, ch), F32)
    pad_ref[half + ny :] = jnp.zeros((half, w, ch), F32)
    pad_ref[half : half + ny] = m_ref[...].astype(F32)
    chunk = min(ny, 8)
    n_chunks = ny // chunk

    def rows_at(y0, lo, hi):
        acc = jnp.zeros((chunk, w, ch), F32)
        for k in range(lo, hi):
            acc = acc + ky_ref[k : k + 1, :][None] * pad_ref[pl.ds(y0 + k, chunk)]
        out_ref[pl.ds(y0, chunk)] = acc.astype(out_ref.dtype)

    if n_chunks <= 8:
        for c in range(n_chunks):
            y0 = c * chunk
            lo = max(0, half - y0 - chunk + 1)
            hi = min(taps, half + ny - y0)
            rows_at(y0, lo, hi)
    else:

        def body(i, carry):
            rows_at(pl.multiple_of(i * chunk, chunk), 0, taps)
            return carry

        lax.fori_loop(0, n_chunks, body, 0)


def meridional(m, ky):
    ny, w, ch = m.shape
    taps = ky.shape[0]
    half = (taps - 1) // 2
    return pl.pallas_call(
        meridional_kernel,
        out_shape=jax.ShapeDtypeStruct(m.shape, BF16),
        in_specs=[VMEM_SPEC] * 2,
        out_specs=VMEM_SPEC,
        scratch_shapes=[pltpu.VMEM((ny + 2 * half, w, ch), F32)],
        compiler_params=SMALL_VMEM,
        cost_estimate=pl.CostEstimate(
            flops=2 * taps * m.size, transcendentals=0, bytes_accessed=4 * m.size
        ),
    )(m, ky)


def per_device(nt, increment, land_sea, kernel_x, kernel_y, balance):
    masked = increment * land_sea.astype(increment.dtype)[:, :, None]
    z = zonal(masked, kernel_x)
    z_other = lax.ppermute(z, "comp", [(0, 1), (1, 0)])
    c = lax.axis_index("comp").astype(jnp.int32).reshape(1)
    mixed = balance_mix(c, z, z_other, balance, land_sea, nt)
    moved = lax.all_to_all(mixed, "tile", split_axis=0, concat_axis=0, tiled=True)
    nt_, rows, width, ch = moved.shape
    return meridional(moved.reshape(nt_ * rows, width, ch), kernel_y)


def solution(mesh):
    nt = mesh.shape["tile"]
    return jax.shard_map(
        functools.partial(per_device, nt),
        mesh=mesh,
        in_specs=(
            P(("ens", "tile"), None, "comp"),
            P("tile", None),
            P(None, "comp"),
            P(None, "comp"),
            P("tile", "comp", None),
        ),
        out_specs=P("ens", "tile", "comp"),
        check_vma=False,
    )
```

```python
import functools

import jax
import jax.numpy as jnp
from jax import lax
from jax.experimental import pallas as pl
from jax.experimental.pallas import tpu as pltpu
from jax.sharding import PartitionSpec as P

F32 = jnp.float32
VMEM_SPEC = pl.BlockSpec(memory_space=pltpu.VMEM)
SMALL_VMEM = pltpu.CompilerParams(vmem_limit_bytes=8 * 1024 * 1024)
BF16 = jnp.bfloat16


def zonal_kernel(m_ref, kx_ref, out_ref, ext_ref):
    rows, nx, ch = m_ref.shape
    taps = kx_ref.shape[0]
    half = (taps - 1) // 2
    pad = ((half + 7) // 8) * 8
    span = nx + 2 * pad - 8
    chunk = min(nx, 64)
    for r in range(rows):
        m = m_ref[r].astype(F32)
        ext = jnp.concatenate([m[nx - pad :], m, m[:pad]], axis=0)
        for s in range(8):
            ext_ref[s] = ext[s : s + span]

        def body(i, carry, r=r):
            x0 = pl.multiple_of(i * chunk, chunk)
            acc = jnp.zeros((chunk, ch), F32)
            for k in range(taps):
                e = k - half + pad
                q, s = divmod(e, 8)
                acc = acc + kx_ref[k : k + 1, :] * ext_ref[s, pl.ds(x0 + 8 * q, chunk), :]
            out_ref[r, pl.ds(x0, chunk), :] = acc.astype(out_ref.dtype)
            return carry

        n_chunks = nx // chunk
        lax.fori_loop(0, n_chunks, body, 0, unroll=n_chunks <= 4)


def zonal(m, kx):
    rows, nx, ch = m.shape
    taps = kx.shape[0]
    pad = (((taps - 1) // 2 + 7) // 8) * 8
    return pl.pallas_call(
        zonal_kernel,
        out_shape=jax.ShapeDtypeStruct(m.shape, BF16),
        in_specs=[VMEM_SPEC] * 2,
        out_specs=VMEM_SPEC,
        scratch_shapes=[pltpu.VMEM((8, nx + 2 * pad - 8, ch), F32)],
        compiler_params=SMALL_VMEM,
        cost_estimate=pl.CostEstimate(
            flops=2 * taps * m.size, transcendentals=0, bytes_accessed=4 * m.size
        ),
    )(m, kx)


def balance_kernel(c_ref, z_ref, zo_ref, b_ref, sea_ref, out_ref, seat_ref):
    nt, rows, width, _ = out_ref.shape
    nx, ch = z_ref.shape[1], z_ref.shape[2]
    sea = sea_ref[...].astype(F32)
    sea_pad = jnp.concatenate([sea, jnp.zeros((128 - rows, nx), F32)], axis=0)
    seat_ref[...] = jnp.transpose(sea_pad)
    c = c_ref[0]
    own = b_ref[0, :, pl.ds(pl.multiple_of(c * ch, ch), ch)]
    other = b_ref[0, :, pl.ds(pl.multiple_of((1 - c) * ch, ch), ch)]
    dims = (((1,), (1,)), ((), ()))
    for r in range(rows):
        res = lax.dot_general(z_ref[r], own, dims, preferred_element_type=F32)
        res = res + lax.dot_general(zo_ref[r], other, dims, preferred_element_type=F32)
        res = (res * seat_ref[:, r : r + 1]).astype(out_ref.dtype)
        for t in range(nt):
            out_ref[t, r] = res[t * width : (t + 1) * width]


def balance_mix(c, z, zo, b, sea, nt):
    rows, nx, ch = z.shape
    ci = b.shape[1]
    return pl.pallas_call(
        balance_kernel,
        out_shape=jax.ShapeDtypeStruct((nt, rows, nx // nt, ci), BF16),
        in_specs=[pl.BlockSpec(memory_space=pltpu.SMEM)] + [VMEM_SPEC] * 4,
        out_specs=VMEM_SPEC,
        scratch_shapes=[pltpu.VMEM((nx, 128), F32)],
        compiler_params=SMALL_VMEM,
        cost_estimate=pl.CostEstimate(
            flops=4 * rows * nx * ch * ci,
            transcendentals=0,
            bytes_accessed=2 * (2 * z.size + b.size + rows * nx * ci),
        ),
    )(c, z, zo, b, sea)


def meridional_kernel(m_ref, ky_ref, out_ref, pad_ref):
    ny, w, ch = m_ref.shape
    taps = ky_ref.shape[0]
    half = (taps - 1) // 2
    chunk = min(ny, 8)
    n_chunks = ny // chunk
    if n_chunks <= 8:
        pad_ref[0:ny] = m_ref[...].astype(F32)
        for c in range(n_chunks):
            y0 = c * chunk
            acc = [None] * chunk
            for k in range(taps):
                d = k - half
                lo, hi = max(0, -d - y0), min(chunk, ny - d - y0)
                if lo >= hi:
                    continue
                term = ky_ref[k : k + 1, :][None] * pad_ref[y0 + d + lo : y0 + d + hi]
                for y in range(lo, hi):
                    acc[y] = term[y - lo] if acc[y] is None else acc[y] + term[y - lo]
            out_ref[y0 : y0 + chunk] = jnp.stack(acc).astype(out_ref.dtype)
        return
    pad_ref[0:half] = jnp.zeros((half, w, ch), F32)
    pad_ref[half + ny :] = jnp.zeros((half, w, ch), F32)
    pad_ref[half : half + ny] = m_ref[...].astype(F32)

    def body(i, carry):
        y0 = pl.multiple_of(i * chunk, chunk)
        acc = jnp.zeros((chunk, w, ch), F32)
        for k in range(taps):
            acc = acc + ky_ref[k : k + 1, :][None] * pad_ref[pl.ds(y0 + k, chunk)]
        out_ref[pl.ds(y0, chunk)] = acc.astype(out_ref.dtype)
        return carry

    lax.fori_loop(0, n_chunks, body, 0)


def meridional(m, ky):
    ny, w, ch = m.shape
    taps = ky.shape[0]
    half = (taps - 1) // 2
    return pl.pallas_call(
        meridional_kernel,
        out_shape=jax.ShapeDtypeStruct(m.shape, BF16),
        in_specs=[VMEM_SPEC] * 2,
        out_specs=VMEM_SPEC,
        scratch_shapes=[pltpu.VMEM((ny + 2 * half, w, ch), F32)],
        compiler_params=SMALL_VMEM,
        cost_estimate=pl.CostEstimate(
            flops=2 * taps * m.size, transcendentals=0, bytes_accessed=4 * m.size
        ),
    )(m, ky)


def per_device(nt, increment, land_sea, kernel_x, kernel_y, balance):
    masked = increment * land_sea.astype(increment.dtype)[:, :, None]
    z = zonal(masked, kernel_x)
    z_other = lax.ppermute(z, "comp", [(0, 1), (1, 0)])
    c = lax.axis_index("comp").astype(jnp.int32).reshape(1)
    mixed = balance_mix(c, z, z_other, balance, land_sea, nt)
    moved = lax.all_to_all(mixed, "tile", split_axis=0, concat_axis=0, tiled=True)
    nt_, rows, width, ch = moved.shape
    return meridional(moved.reshape(nt_ * rows, width, ch), kernel_y)


def solution(mesh):
    nt = mesh.shape["tile"]
    return jax.shard_map(
        functools.partial(per_device, nt),
        mesh=mesh,
        in_specs=(
            P(("ens", "tile"), None, "comp"),
            P("tile", None),
            P(None, "comp"),
            P(None, "comp"),
            P("tile", "comp", None),
        ),
        out_specs=P("ens", "tile", "comp"),
        check_vma=False,
    )
```

```python
import functools

import jax
import jax.numpy as jnp
from jax import lax
from jax.experimental import pallas as pl
from jax.experimental.pallas import tpu as pltpu
from jax.sharding import PartitionSpec as P

F32 = jnp.float32
VMEM_SPEC = pl.BlockSpec(memory_space=pltpu.VMEM)
SMALL_VMEM = pltpu.CompilerParams(vmem_limit_bytes=8 * 1024 * 1024)
BF16 = jnp.bfloat16


def zonal_kernel(m_ref, kx_ref, out_ref, ext_ref):
    rows, nx, ch = m_ref.shape
    taps = kx_ref.shape[0]
    half = (taps - 1) // 2
    pad = ((half + 7) // 8) * 8
    span = nx + 2 * pad - 8
    chunk = min(nx, 64)
    for r in range(rows):
        m = m_ref[r].astype(F32)
        ext = jnp.concatenate([m[nx - pad :], m, m[:pad]], axis=0)
        for s in range(8):
            ext_ref[s] = ext[s : s + span]

        def body(i, carry, r=r):
            x0 = pl.multiple_of(i * chunk, chunk)
            acc = jnp.zeros((chunk, ch), F32)
            for k in range(taps):
                e = k - half + pad
                q, s = divmod(e, 8)
                acc = acc + kx_ref[k : k + 1, :] * ext_ref[s, pl.ds(x0 + 8 * q, chunk), :]
            out_ref[r, pl.ds(x0, chunk), :] = acc.astype(out_ref.dtype)
            return carry

        n_chunks = nx // chunk
        lax.fori_loop(0, n_chunks, body, 0, unroll=n_chunks <= 4)


def zonal(m, kx):
    rows, nx, ch = m.shape
    taps = kx.shape[0]
    pad = (((taps - 1) // 2 + 7) // 8) * 8
    return pl.pallas_call(
        zonal_kernel,
        out_shape=jax.ShapeDtypeStruct(m.shape, BF16),
        in_specs=[VMEM_SPEC] * 2,
        out_specs=VMEM_SPEC,
        scratch_shapes=[pltpu.VMEM((8, nx + 2 * pad - 8, ch), F32)],
        compiler_params=SMALL_VMEM,
        cost_estimate=pl.CostEstimate(
            flops=2 * taps * m.size, transcendentals=0, bytes_accessed=4 * m.size
        ),
    )(m, kx)


def balance_kernel(c_ref, z_ref, zo_ref, b_ref, sea_ref, out_ref, seat_ref):
    nt, rows, width, _ = out_ref.shape
    nx, ch = z_ref.shape[1], z_ref.shape[2]
    sea = sea_ref[...].astype(F32)
    sea_pad = jnp.concatenate([sea, jnp.zeros((128 - rows, nx), F32)], axis=0)
    seat_ref[...] = jnp.transpose(sea_pad)
    c = c_ref[0]
    own = b_ref[0, :, pl.ds(pl.multiple_of(c * ch, ch), ch)]
    other = b_ref[0, :, pl.ds(pl.multiple_of((1 - c) * ch, ch), ch)]
    dims = (((1,), (1,)), ((), ()))
    for r in range(rows):
        res = lax.dot_general(z_ref[r], own, dims, preferred_element_type=F32)
        res = res + lax.dot_general(zo_ref[r], other, dims, preferred_element_type=F32)
        res = (res * seat_ref[:, r : r + 1]).astype(out_ref.dtype)
        for t in range(nt):
            out_ref[t, r] = res[t * width : (t + 1) * width]


def balance_mix(c, z, zo, b, sea, nt):
    rows, nx, ch = z.shape
    ci = b.shape[1]
    return pl.pallas_call(
        balance_kernel,
        out_shape=jax.ShapeDtypeStruct((nt, rows, nx // nt, ci), BF16),
        in_specs=[pl.BlockSpec(memory_space=pltpu.SMEM)] + [VMEM_SPEC] * 4,
        out_specs=VMEM_SPEC,
        scratch_shapes=[pltpu.VMEM((nx, 128), F32)],
        compiler_params=SMALL_VMEM,
        cost_estimate=pl.CostEstimate(
            flops=4 * rows * nx * ch * ci,
            transcendentals=0,
            bytes_accessed=2 * (2 * z.size + b.size + rows * nx * ci),
        ),
    )(c, z, zo, b, sea)


def meridional_kernel(m_ref, ky_ref, out_hbm, pad_ref, res_ref, sems):
    ny, w, ch = m_ref.shape
    taps = ky_ref.shape[0]
    half = (taps - 1) // 2
    chunk = min(ny, 8)
    n_chunks = ny // chunk
    if n_chunks <= 8:
        pad_ref[0:ny] = m_ref[...].astype(F32)
        copies = []
        for c in range(n_chunks):
            y0 = c * chunk
            acc = [None] * chunk
            for k in range(taps):
                d = k - half
                lo, hi = max(0, -d - y0), min(chunk, ny - d - y0)
                if lo >= hi:
                    continue
                term = ky_ref[k : k + 1, :][None] * pad_ref[y0 + d + lo : y0 + d + hi]
                for y in range(lo, hi):
                    acc[y] = term[y - lo] if acc[y] is None else acc[y] + term[y - lo]
            res_ref[y0 : y0 + chunk] = jnp.stack(acc).astype(res_ref.dtype)
            copy = pltpu.make_async_copy(res_ref.at[y0 : y0 + chunk], out_hbm.at[y0 : y0 + chunk], sems.at[c])
            copy.start()
            copies.append(copy)
        for copy in copies:
            copy.wait()
        return
    pad_ref[0:half] = jnp.zeros((half, w, ch), F32)
    pad_ref[half + ny :] = jnp.zeros((half, w, ch), F32)
    pad_ref[half : half + ny] = m_ref[...].astype(F32)

    def body(i, carry):
        y0 = pl.multiple_of(i * chunk, chunk)
        acc = jnp.zeros((chunk, w, ch), F32)
        for k in range(taps):
            acc = acc + ky_ref[k : k + 1, :][None] * pad_ref[pl.ds(y0 + k, chunk)]
        res_ref[pl.ds(y0, chunk)] = acc.astype(res_ref.dtype)
        return carry

    lax.fori_loop(0, n_chunks, body, 0)
    copy = pltpu.make_async_copy(res_ref, out_hbm, sems.at[0])
    copy.start()
    copy.wait()


def meridional(m, ky):
    ny, w, ch = m.shape
    taps = ky.shape[0]
    half = (taps - 1) // 2
    n_chunks = ny // min(ny, 8)
    return pl.pallas_call(
        meridional_kernel,
        out_shape=jax.ShapeDtypeStruct(m.shape, BF16),
        in_specs=[VMEM_SPEC] * 2,
        out_specs=pl.BlockSpec(memory_space=pl.ANY),
        scratch_shapes=[
            pltpu.VMEM((ny + 2 * half, w, ch), F32),
            pltpu.VMEM(m.shape, BF16),
            pltpu.SemaphoreType.DMA((n_chunks,)),
        ],
        compiler_params=SMALL_VMEM,
        cost_estimate=pl.CostEstimate(
            flops=2 * taps * m.size, transcendentals=0, bytes_accessed=4 * m.size
        ),
    )(m, ky)


def per_device(nt, increment, land_sea, kernel_x, kernel_y, balance):
    masked = increment * land_sea.astype(increment.dtype)[:, :, None]
    z = zonal(masked, kernel_x)
    z_other = lax.ppermute(z, "comp", [(0, 1), (1, 0)])
    c = lax.axis_index("comp").astype(jnp.int32).reshape(1)
    mixed = balance_mix(c, z, z_other, balance, land_sea, nt)
    moved = lax.all_to_all(mixed, "tile", split_axis=0, concat_axis=0, tiled=True)
    nt_, rows, width, ch = moved.shape
    return meridional(moved.reshape(nt_ * rows, width, ch), kernel_y)


def solution(mesh):
    nt = mesh.shape["tile"]
    return jax.shard_map(
        functools.partial(per_device, nt),
        mesh=mesh,
        in_specs=(
            P(("ens", "tile"), None, "comp"),
            P("tile", None),
            P(None, "comp"),
            P(None, "comp"),
            P("tile", "comp", None),
        ),
        out_specs=P("ens", "tile", "comp"),
        check_vma=False,
    )
```

```python
import functools

import jax
import jax.numpy as jnp
from jax import lax
from jax.experimental import pallas as pl
from jax.experimental.pallas import tpu as pltpu
from jax.sharding import PartitionSpec as P

F32 = jnp.float32
VMEM_SPEC = pl.BlockSpec(memory_space=pltpu.VMEM)
SMALL_VMEM = pltpu.CompilerParams(vmem_limit_bytes=8 * 1024 * 1024)
BF16 = jnp.bfloat16


def zonal_kernel(m_ref, kx_ref, out_ref, ext_ref):
    rows, nx, ch = m_ref.shape
    taps = kx_ref.shape[0]
    half = (taps - 1) // 2
    pad = ((half + 7) // 8) * 8
    span = nx + 2 * pad - 8
    chunk = min(nx, 64)
    for r in range(rows):
        m = m_ref[r].astype(F32)
        ext = jnp.concatenate([m[nx - pad :], m, m[:pad]], axis=0)
        for s in range(8):
            ext_ref[s] = ext[s : s + span]

        def body(i, carry, r=r):
            x0 = pl.multiple_of(i * chunk, chunk)
            acc = jnp.zeros((chunk, ch), F32)
            for k in range(taps):
                e = k - half + pad
                q, s = divmod(e, 8)
                acc = acc + kx_ref[k : k + 1, :] * ext_ref[s, pl.ds(x0 + 8 * q, chunk), :]
            out_ref[r, pl.ds(x0, chunk), :] = acc.astype(out_ref.dtype)
            return carry

        n_chunks = nx // chunk
        lax.fori_loop(0, n_chunks, body, 0, unroll=n_chunks <= 4)


def zonal(m, kx):
    rows, nx, ch = m.shape
    taps = kx.shape[0]
    pad = (((taps - 1) // 2 + 7) // 8) * 8
    return pl.pallas_call(
        zonal_kernel,
        out_shape=jax.ShapeDtypeStruct(m.shape, BF16),
        in_specs=[VMEM_SPEC] * 2,
        out_specs=VMEM_SPEC,
        scratch_shapes=[pltpu.VMEM((8, nx + 2 * pad - 8, ch), F32)],
        compiler_params=SMALL_VMEM,
        cost_estimate=pl.CostEstimate(
            flops=2 * taps * m.size, transcendentals=0, bytes_accessed=4 * m.size
        ),
    )(m, kx)


def own_half_kernel(c_ref, z_ref, b_ref, out_ref):
    rows, _, ch = z_ref.shape
    c = c_ref[0]
    own = b_ref[0, :, pl.ds(pl.multiple_of(c * ch, ch), ch)]
    for r in range(rows):
        out_ref[r] = lax.dot_general(z_ref[r], own, (((1,), (1,)), ((), ())), preferred_element_type=F32)


def balance_kernel(c_ref, p_ref, zo_ref, b_ref, sea_ref, out_ref, seat_ref):
    nt, rows, width, _ = out_ref.shape
    nx, ch = zo_ref.shape[1], zo_ref.shape[2]
    sea = sea_ref[...].astype(F32)
    sea_pad = jnp.concatenate([sea, jnp.zeros((128 - rows, nx), F32)], axis=0)
    seat_ref[...] = jnp.transpose(sea_pad)
    c = c_ref[0]
    other = b_ref[0, :, pl.ds(pl.multiple_of((1 - c) * ch, ch), ch)]
    dims = (((1,), (1,)), ((), ()))
    for r in range(rows):
        res = p_ref[r] + lax.dot_general(zo_ref[r], other, dims, preferred_element_type=F32)
        res = (res * seat_ref[:, r : r + 1]).astype(out_ref.dtype)
        for t in range(nt):
            out_ref[t, r] = res[t * width : (t + 1) * width]


def balance_mix(c, z, zo, b, sea, nt):
    rows, nx, ch = z.shape
    ci = b.shape[1]
    smem = pl.BlockSpec(memory_space=pltpu.SMEM)
    partial = pl.pallas_call(
        own_half_kernel,
        out_shape=jax.ShapeDtypeStruct((rows, nx, ci), F32),
        in_specs=[smem] + [VMEM_SPEC] * 2,
        out_specs=VMEM_SPEC,
        compiler_params=SMALL_VMEM,
        cost_estimate=pl.CostEstimate(
            flops=2 * rows * nx * ch * ci,
            transcendentals=0,
            bytes_accessed=2 * (z.size + b.size) + 4 * rows * nx * ci,
        ),
    )(c, z, b)
    return pl.pallas_call(
        balance_kernel,
        out_shape=jax.ShapeDtypeStruct((nt, rows, nx // nt, ci), BF16),
        in_specs=[smem] + [VMEM_SPEC] * 4,
        out_specs=VMEM_SPEC,
        scratch_shapes=[pltpu.VMEM((nx, 128), F32)],
        compiler_params=SMALL_VMEM,
        cost_estimate=pl.CostEstimate(
            flops=2 * rows * nx * ch * ci,
            transcendentals=0,
            bytes_accessed=2 * (zo.size + b.size + rows * nx * ci) + 4 * rows * nx * ci,
        ),
    )(c, partial, zo, b, sea)


def meridional_kernel(m_ref, ky_ref, out_ref, pad_ref):
    ny, w, ch = m_ref.shape
    taps = ky_ref.shape[0]
    half = (taps - 1) // 2
    chunk = min(ny, 8)
    n_chunks = ny // chunk
    if n_chunks <= 8:
        pad_ref[0:ny] = m_ref[...].astype(F32)
        for c in range(n_chunks):
            y0 = c * chunk
            acc = [None] * chunk
            for k in range(taps):
                d = k - half
                lo, hi = max(0, -d - y0), min(chunk, ny - d - y0)
                if lo >= hi:
                    continue
                term = ky_ref[k : k + 1, :][None] * pad_ref[y0 + d + lo : y0 + d + hi]
                for y in range(lo, hi):
                    acc[y] = term[y - lo] if acc[y] is None else acc[y] + term[y - lo]
            out_ref[y0 : y0 + chunk] = jnp.stack(acc).astype(out_ref.dtype)
        return
    pad_ref[0:half] = jnp.zeros((half, w, ch), F32)
    pad_ref[half + ny :] = jnp.zeros((half, w, ch), F32)
    pad_ref[half : half + ny] = m_ref[...].astype(F32)

    def body(i, carry):
        y0 = pl.multiple_of(i * chunk, chunk)
        acc = jnp.zeros((chunk, w, ch), F32)
        for k in range(taps):
            acc = acc + ky_ref[k : k + 1, :][None] * pad_ref[pl.ds(y0 + k, chunk)]
        out_ref[pl.ds(y0, chunk)] = acc.astype(out_ref.dtype)
        return carry

    lax.fori_loop(0, n_chunks, body, 0)


def meridional(m, ky):
    ny, w, ch = m.shape
    taps = ky.shape[0]
    half = (taps - 1) // 2
    return pl.pallas_call(
        meridional_kernel,
        out_shape=jax.ShapeDtypeStruct(m.shape, BF16),
        in_specs=[VMEM_SPEC] * 2,
        out_specs=VMEM_SPEC,
        scratch_shapes=[pltpu.VMEM((ny + 2 * half, w, ch), F32)],
        compiler_params=SMALL_VMEM,
        cost_estimate=pl.CostEstimate(
            flops=2 * taps * m.size, transcendentals=0, bytes_accessed=4 * m.size
        ),
    )(m, ky)


def per_device(nt, increment, land_sea, kernel_x, kernel_y, balance):
    masked = increment * land_sea.astype(increment.dtype)[:, :, None]
    z = zonal(masked, kernel_x)
    z_other = lax.ppermute(z, "comp", [(0, 1), (1, 0)])
    c = lax.axis_index("comp").astype(jnp.int32).reshape(1)
    mixed = balance_mix(c, z, z_other, balance, land_sea, nt)
    moved = lax.all_to_all(mixed, "tile", split_axis=0, concat_axis=0, tiled=True)
    nt_, rows, width, ch = moved.shape
    return meridional(moved.reshape(nt_ * rows, width, ch), kernel_y)


def solution(mesh):
    nt = mesh.shape["tile"]
    return jax.shard_map(
        functools.partial(per_device, nt),
        mesh=mesh,
        in_specs=(
            P(("ens", "tile"), None, "comp"),
            P("tile", None),
            P(None, "comp"),
            P(None, "comp"),
            P("tile", "comp", None),
        ),
        out_specs=P("ens", "tile", "comp"),
        check_vma=False,
    )
```

```python
import functools

import jax
import jax.numpy as jnp
from jax import lax
from jax.experimental import pallas as pl
from jax.experimental.pallas import tpu as pltpu
from jax.sharding import PartitionSpec as P

F32 = jnp.float32
VMEM_SPEC = pl.BlockSpec(memory_space=pltpu.VMEM)
SMALL_VMEM = pltpu.CompilerParams(vmem_limit_bytes=8 * 1024 * 1024)
BF16 = jnp.bfloat16


def zonal_rows(m_of, kx_ref, store, ext_ref, rows, nx, ch):
    taps = kx_ref.shape[0]
    half = (taps - 1) // 2
    pad = ((half + 7) // 8) * 8
    span = nx + 2 * pad - 8
    chunk = min(nx, 64)
    for r in range(rows):
        m = m_of(r)
        ext = jnp.concatenate([m[nx - pad :], m, m[:pad]], axis=0)
        for s in range(8):
            ext_ref[s] = ext[s : s + span]

        def body(i, carry, r=r):
            x0 = pl.multiple_of(i * chunk, chunk)
            acc = jnp.zeros((chunk, ch), F32)
            for k in range(taps):
                e = k - half + pad
                q, s = divmod(e, 8)
                acc = acc + kx_ref[k : k + 1, :] * ext_ref[s, pl.ds(x0 + 8 * q, chunk), :]
            store(r, x0, chunk, acc)
            return carry

        n_chunks = nx // chunk
        lax.fori_loop(0, n_chunks, body, 0, unroll=n_chunks <= 4)


def ext_shape(nx, ch, taps):
    pad = (((taps - 1) // 2 + 7) // 8) * 8
    return (8, nx + 2 * pad - 8, ch)


def zonal_kernel(m_ref, kx_ref, out_ref, ext_ref):
    rows, nx, ch = m_ref.shape

    def store(r, x0, chunk, acc):
        out_ref[r, pl.ds(x0, chunk), :] = acc.astype(out_ref.dtype)

    zonal_rows(lambda r: m_ref[r].astype(F32), kx_ref, store, ext_ref, rows, nx, ch)


def zonal(m, kx):
    rows, nx, ch = m.shape
    taps = kx.shape[0]
    return pl.pallas_call(
        zonal_kernel,
        out_shape=jax.ShapeDtypeStruct(m.shape, BF16),
        in_specs=[VMEM_SPEC] * 2,
        out_specs=VMEM_SPEC,
        scratch_shapes=[pltpu.VMEM(ext_shape(nx, ch, taps), F32)],
        compiler_params=SMALL_VMEM,
        cost_estimate=pl.CostEstimate(
            flops=2 * taps * m.size, transcendentals=0, bytes_accessed=4 * m.size
        ),
    )(m, kx)


def balance_kernel(c_ref, z_ref, io_ref, kxo_ref, b_ref, sea_ref, out_ref, zo_ref, ext_ref, seat_ref):
    nt, rows, width, _ = out_ref.shape
    nx, ch = z_ref.shape[1], z_ref.shape[2]
    sea = sea_ref[...].astype(F32)
    sea_pad = jnp.concatenate([sea, jnp.zeros((128 - rows, nx), F32)], axis=0)
    seat_ref[...] = jnp.transpose(sea_pad)

    def store(r, x0, chunk, acc):
        zo_ref[r, pl.ds(x0, chunk), :] = acc.astype(zo_ref.dtype)

    zonal_rows(
        lambda r: io_ref[r].astype(F32) * seat_ref[:, r : r + 1], kxo_ref, store, ext_ref, rows, nx, ch
    )
    c = c_ref[0]
    own = b_ref[0, :, pl.ds(pl.multiple_of(c * ch, ch), ch)]
    other = b_ref[0, :, pl.ds(pl.multiple_of((1 - c) * ch, ch), ch)]
    dims = (((1,), (1,)), ((), ()))
    for r in range(rows):
        res = lax.dot_general(z_ref[r], own, dims, preferred_element_type=F32)
        res = res + lax.dot_general(zo_ref[r], other, dims, preferred_element_type=F32)
        res = (res * seat_ref[:, r : r + 1]).astype(out_ref.dtype)
        for t in range(nt):
            out_ref[t, r] = res[t * width : (t + 1) * width]


def balance_mix(c, z, io, kxo, b, sea, nt):
    rows, nx, ch = z.shape
    ci = b.shape[1]
    taps = kxo.shape[0]
    return pl.pallas_call(
        balance_kernel,
        out_shape=jax.ShapeDtypeStruct((nt, rows, nx // nt, ci), BF16),
        in_specs=[pl.BlockSpec(memory_space=pltpu.SMEM)] + [VMEM_SPEC] * 5,
        out_specs=VMEM_SPEC,
        scratch_shapes=[
            pltpu.VMEM(z.shape, BF16),
            pltpu.VMEM(ext_shape(nx, ch, taps), F32),
            pltpu.VMEM((nx, 128), F32),
        ],
        compiler_params=SMALL_VMEM,
        cost_estimate=pl.CostEstimate(
            flops=4 * rows * nx * ch * ci + 2 * taps * z.size,
            transcendentals=0,
            bytes_accessed=2 * (2 * z.size + b.size + rows * nx * ci),
        ),
    )(c, z, io, kxo, b, sea)


def meridional_kernel(m_ref, ky_ref, out_ref, pad_ref):
    ny, w, ch = m_ref.shape
    taps = ky_ref.shape[0]
    half = (taps - 1) // 2
    pad_ref[0:half] = jnp.zeros((half, w, ch), F32)
    pad_ref[half + ny :] = jnp.zeros((half, w, ch), F32)
    pad_ref[half : half + ny] = m_ref[...].astype(F32)
    chunk = min(ny, 8)
    n_chunks = ny // chunk

    def rows_at(y0, lo, hi):
        acc = jnp.zeros((chunk, w, ch), F32)
        for k in range(lo, hi):
            acc = acc + ky_ref[k : k + 1, :][None] * pad_ref[pl.ds(y0 + k, chunk)]
        out_ref[pl.ds(y0, chunk)] = acc.astype(out_ref.dtype)

    if n_chunks <= 8:
        for c in range(n_chunks):
            y0 = c * chunk
            lo = max(0, half - y0 - chunk + 1)
            hi = min(taps, half + ny - y0)
            rows_at(y0, lo, hi)
    else:

        def body(i, carry):
            rows_at(pl.multiple_of(i * chunk, chunk), 0, taps)
            return carry

        lax.fori_loop(0, n_chunks, body, 0)


def meridional(m, ky):
    ny, w, ch = m.shape
    taps = ky.shape[0]
    half = (taps - 1) // 2
    return pl.pallas_call(
        meridional_kernel,
        out_shape=jax.ShapeDtypeStruct(m.shape, BF16),
        in_specs=[VMEM_SPEC] * 2,
        out_specs=VMEM_SPEC,
        scratch_shapes=[pltpu.VMEM((ny + 2 * half, w, ch), F32)],
        compiler_params=SMALL_VMEM,
        cost_estimate=pl.CostEstimate(
            flops=2 * taps * m.size, transcendentals=0, bytes_accessed=4 * m.size
        ),
    )(m, ky)


def per_device(nt, increment, land_sea, kernel_x, kernel_y, balance):
    inc_other, kx_other = lax.ppermute((increment, kernel_x), "comp", [(0, 1), (1, 0)])
    masked = increment * land_sea.astype(increment.dtype)[:, :, None]
    z = zonal(masked, kernel_x)
    c = lax.axis_index("comp").astype(jnp.int32).reshape(1)
    mixed = balance_mix(c, z, inc_other, kx_other, balance, land_sea, nt)
    moved = lax.all_to_all(mixed, "tile", split_axis=0, concat_axis=0, tiled=True)
    nt_, rows, width, ch = moved.shape
    return meridional(moved.reshape(nt_ * rows, width, ch), kernel_y)


def solution(mesh):
    nt = mesh.shape["tile"]
    return jax.shard_map(
        functools.partial(per_device, nt),
        mesh=mesh,
        in_specs=(
            P(("ens", "tile"), None, "comp"),
            P("tile", None),
            P(None, "comp"),
            P(None, "comp"),
            P("tile", "comp", None),
        ),
        out_specs=P("ens", "tile", "comp"),
        check_vma=False,
    )
```

```python
import functools

import jax
import jax.numpy as jnp
from jax import lax
from jax.experimental import pallas as pl
from jax.experimental.pallas import tpu as pltpu
from jax.sharding import PartitionSpec as P

F32 = jnp.float32
VMEM_SPEC = pl.BlockSpec(memory_space=pltpu.VMEM)
SMALL_VMEM = pltpu.CompilerParams(vmem_limit_bytes=8 * 1024 * 1024)
BF16 = jnp.bfloat16


def zonal_kernel(m_ref, kx_ref, out_ref, ext_ref):
    rows, nx, ch = m_ref.shape
    taps = kx_ref.shape[0]
    half = (taps - 1) // 2
    pad = ((half + 7) // 8) * 8
    span = nx + 2 * pad - 8
    chunk = min(nx, 64)
    for r in range(rows):
        m = m_ref[r].astype(F32)
        ext = jnp.concatenate([m[nx - pad :], m, m[:pad]], axis=0)
        for s in range(8):
            ext_ref[s] = ext[s : s + span]

        def body(i, carry, r=r):
            x0 = pl.multiple_of(i * chunk, chunk)
            acc = jnp.zeros((chunk, ch), F32)
            for k in range(taps):
                e = k - half + pad
                q, s = divmod(e, 8)
                acc = acc + kx_ref[k : k + 1, :] * ext_ref[s, pl.ds(x0 + 8 * q, chunk), :]
            out_ref[r, pl.ds(x0, chunk), :] = acc.astype(out_ref.dtype)
            return carry

        n_chunks = nx // chunk
        lax.fori_loop(0, n_chunks, body, 0, unroll=n_chunks <= 4)


def zonal(m, kx):
    rows, nx, ch = m.shape
    taps = kx.shape[0]
    pad = (((taps - 1) // 2 + 7) // 8) * 8
    return pl.pallas_call(
        zonal_kernel,
        out_shape=jax.ShapeDtypeStruct(m.shape, BF16),
        in_specs=[VMEM_SPEC] * 2,
        out_specs=VMEM_SPEC,
        scratch_shapes=[pltpu.VMEM((8, nx + 2 * pad - 8, ch), F32)],
        compiler_params=SMALL_VMEM,
        cost_estimate=pl.CostEstimate(
            flops=2 * taps * m.size, transcendentals=0, bytes_accessed=4 * m.size
        ),
    )(m, kx)


def balance_kernel(c_ref, z_ref, zo_ref, b_ref, sea_ref, out_ref, seat_ref):
    nt, rows, width, _ = out_ref.shape
    nx, ch = z_ref.shape[1], z_ref.shape[2]
    sea = sea_ref[...].astype(F32)
    sea_pad = jnp.concatenate([sea, jnp.zeros((128 - rows, nx), F32)], axis=0)
    seat_ref[...] = jnp.transpose(sea_pad)
    c = c_ref[0]
    own = b_ref[0, :, pl.ds(pl.multiple_of(c * ch, ch), ch)]
    other = b_ref[0, :, pl.ds(pl.multiple_of((1 - c) * ch, ch), ch)]
    dims = (((1,), (1,)), ((), ()))
    for r in range(rows):
        res = lax.dot_general(z_ref[r], own, dims, preferred_element_type=F32)
        res = res + lax.dot_general(zo_ref[r], other, dims, preferred_element_type=F32)
        res = (res * seat_ref[:, r : r + 1]).astype(out_ref.dtype)
        for t in range(nt):
            out_ref[t, r] = res[t * width : (t + 1) * width]


def balance_mix(c, z, zo, b, sea, nt):
    rows, nx, ch = z.shape
    ci = b.shape[1]
    return pl.pallas_call(
        balance_kernel,
        out_shape=jax.ShapeDtypeStruct((nt, rows, nx // nt, ci), BF16),
        in_specs=[pl.BlockSpec(memory_space=pltpu.SMEM)] + [VMEM_SPEC] * 4,
        out_specs=VMEM_SPEC,
        scratch_shapes=[pltpu.VMEM((nx, 128), F32)],
        compiler_params=SMALL_VMEM,
        cost_estimate=pl.CostEstimate(
            flops=4 * rows * nx * ch * ci,
            transcendentals=0,
            bytes_accessed=2 * (2 * z.size + b.size + rows * nx * ci),
        ),
    )(c, z, zo, b, sea)


def meridional_kernel(m_ref, ky_ref, out_ref, pad_ref):
    ny, w, ch = m_ref.shape
    taps = ky_ref.shape[0]
    half = (taps - 1) // 2
    pad_ref[0:half] = jnp.zeros((half, w, ch), F32)
    pad_ref[half + ny :] = jnp.zeros((half, w, ch), F32)
    pad_ref[half : half + ny] = m_ref[...].astype(F32)
    chunk = min(ny, 8)
    n_chunks = ny // chunk

    def rows_at(y0, lo, hi):
        acc = jnp.zeros((chunk, w, ch), F32)
        for k in range(lo, hi):
            acc = acc + ky_ref[k : k + 1, :][None] * pad_ref[pl.ds(y0 + k, chunk)]
        out_ref[pl.ds(y0, chunk)] = acc.astype(out_ref.dtype)

    if n_chunks <= 8:
        for c in range(n_chunks):
            y0 = c * chunk
            lo = max(0, half - y0 - chunk + 1)
            hi = min(taps, half + ny - y0)
            rows_at(y0, lo, hi)
    else:

        def body(i, carry):
            rows_at(pl.multiple_of(i * chunk, chunk), 0, taps)
            return carry

        lax.fori_loop(0, n_chunks, body, 0)


def meridional(m, ky):
    ny, w, ch = m.shape
    taps = ky.shape[0]
    half = (taps - 1) // 2
    return pl.pallas_call(
        meridional_kernel,
        out_shape=jax.ShapeDtypeStruct(m.shape, BF16),
        in_specs=[VMEM_SPEC] * 2,
        out_specs=VMEM_SPEC,
        scratch_shapes=[pltpu.VMEM((ny + 2 * half, w, ch), F32)],
        compiler_params=SMALL_VMEM,
        cost_estimate=pl.CostEstimate(
            flops=2 * taps * m.size, transcendentals=0, bytes_accessed=4 * m.size
        ),
    )(m, ky)


def per_device(nt, increment, land_sea, kernel_x, kernel_y, balance):
    rows, nx, _ = increment.shape
    on_diagonal = lax.broadcasted_iota(jnp.int32, (rows, nx, nx), 1) == lax.broadcasted_iota(jnp.int32, (rows, nx, nx), 2)
    diag = jnp.where(on_diagonal, land_sea[:, :, None], 0).astype(increment.dtype)
    masked = jnp.einsum("rxy,ryc->rxc", diag, increment, preferred_element_type=F32).astype(increment.dtype)
    z = zonal(masked, kernel_x)
    z_other = lax.ppermute(z, "comp", [(0, 1), (1, 0)])
    c = lax.axis_index("comp").astype(jnp.int32).reshape(1)
    mixed = balance_mix(c, z, z_other, balance, land_sea, nt)
    moved = lax.all_to_all(mixed, "tile", split_axis=0, concat_axis=0, tiled=True)
    nt_, rows, width, ch = moved.shape
    return meridional(moved.reshape(nt_ * rows, width, ch), kernel_y)


def solution(mesh):
    nt = mesh.shape["tile"]
    return jax.shard_map(
        functools.partial(per_device, nt),
        mesh=mesh,
        in_specs=(
            P(("ens", "tile"), None, "comp"),
            P("tile", None),
            P(None, "comp"),
            P(None, "comp"),
            P("tile", "comp", None),
        ),
        out_specs=P("ens", "tile", "comp"),
        check_vma=False,
    )
```

```python
import functools

import jax
import jax.numpy as jnp
from jax import lax
from jax.experimental import pallas as pl
from jax.experimental.pallas import tpu as pltpu
from jax.sharding import PartitionSpec as P

F32 = jnp.float32
VMEM_SPEC = pl.BlockSpec(memory_space=pltpu.VMEM)
SMALL_VMEM = pltpu.CompilerParams(vmem_limit_bytes=8 * 1024 * 1024)
BF16 = jnp.bfloat16


def zonal_kernel(m_ref, kx_ref, out_ref, ext_ref):
    rows, nx, ch = m_ref.shape
    taps = kx_ref.shape[0]
    half = (taps - 1) // 2
    pad = ((half + 7) // 8) * 8
    span = nx + 2 * pad - 8
    chunk = min(nx, 64)
    for r in range(rows):
        m = m_ref[r].astype(F32)
        ext = jnp.concatenate([m[nx - pad :], m, m[:pad]], axis=0)
        for s in range(8):
            ext_ref[s] = ext[s : s + span]

        def body(i, carry, r=r):
            x0 = pl.multiple_of(i * chunk, chunk)
            acc = jnp.zeros((chunk, ch), F32)
            for k in range(taps):
                e = k - half + pad
                q, s = divmod(e, 8)
                acc = acc + kx_ref[k : k + 1, :] * ext_ref[s, pl.ds(x0 + 8 * q, chunk), :]
            out_ref[r, pl.ds(x0, chunk), :] = acc.astype(out_ref.dtype)
            return carry

        n_chunks = nx // chunk
        lax.fori_loop(0, n_chunks, body, 0, unroll=n_chunks <= 4)


def zonal(m, kx):
    rows, nx, ch = m.shape
    taps = kx.shape[0]
    pad = (((taps - 1) // 2 + 7) // 8) * 8
    return pl.pallas_call(
        zonal_kernel,
        out_shape=jax.ShapeDtypeStruct(m.shape, BF16),
        in_specs=[VMEM_SPEC] * 2,
        out_specs=VMEM_SPEC,
        scratch_shapes=[pltpu.VMEM((8, nx + 2 * pad - 8, ch), F32)],
        compiler_params=SMALL_VMEM,
        cost_estimate=pl.CostEstimate(
            flops=2 * taps * m.size, transcendentals=0, bytes_accessed=4 * m.size
        ),
    )(m, kx)


def balance_kernel(c_ref, z_ref, zo_ref, b_ref, sea_ref, out_ref, seat_ref):
    nt, rows, width, _ = out_ref.shape
    nx, ch = z_ref.shape[1], z_ref.shape[2]
    sea = sea_ref[...].astype(F32)
    sea_pad = jnp.concatenate([sea, jnp.zeros((128 - rows, nx), F32)], axis=0)
    seat_ref[...] = jnp.transpose(sea_pad)
    c = c_ref[0]
    own = b_ref[0, :, pl.ds(pl.multiple_of(c * ch, ch), ch)]
    other = b_ref[0, :, pl.ds(pl.multiple_of((1 - c) * ch, ch), ch)]
    dims = (((1,), (1,)), ((), ()))
    for r in range(rows):
        res = lax.dot_general(z_ref[r], own, dims, preferred_element_type=F32)
        res = res + lax.dot_general(zo_ref[r], other, dims, preferred_element_type=F32)
        res = (res * seat_ref[:, r : r + 1]).astype(out_ref.dtype)
        for t in range(nt):
            out_ref[t, r] = res[t * width : (t + 1) * width]


def balance_mix(c, z, zo, b, sea, nt):
    rows, nx, ch = z.shape
    ci = b.shape[1]
    return pl.pallas_call(
        balance_kernel,
        out_shape=jax.ShapeDtypeStruct((nt, rows, nx // nt, ci), BF16),
        in_specs=[pl.BlockSpec(memory_space=pltpu.SMEM)] + [VMEM_SPEC] * 4,
        out_specs=VMEM_SPEC,
        scratch_shapes=[pltpu.VMEM((nx, 128), F32)],
        compiler_params=SMALL_VMEM,
        cost_estimate=pl.CostEstimate(
            flops=4 * rows * nx * ch * ci,
            transcendentals=0,
            bytes_accessed=2 * (2 * z.size + b.size + rows * nx * ci),
        ),
    )(c, z, zo, b, sea)


def meridional_kernel(m_ref, ky_ref, out_ref, pad_ref):
    ny, w, ch = m_ref.shape
    taps = ky_ref.shape[0]
    half = (taps - 1) // 2
    pad_ref[0:half] = jnp.zeros((half, w, ch), F32)
    pad_ref[half + ny :] = jnp.zeros((half, w, ch), F32)
    pad_ref[half : half + ny] = m_ref[...].astype(F32)
    chunk = min(ny, 8)
    n_chunks = ny // chunk

    def rows_at(y0, lo, hi):
        acc = jnp.zeros((chunk, w, ch), F32)
        for k in range(lo, hi):
            acc = acc + ky_ref[k : k + 1, :][None] * pad_ref[pl.ds(y0 + k, chunk)]
        out_ref[pl.ds(y0, chunk)] = acc.astype(out_ref.dtype)

    if n_chunks <= 8:
        for c in range(n_chunks):
            y0 = c * chunk
            lo = max(0, half - y0 - chunk + 1)
            hi = min(taps, half + ny - y0)
            rows_at(y0, lo, hi)
    else:

        def body(i, carry):
            rows_at(pl.multiple_of(i * chunk, chunk), 0, taps)
            return carry

        lax.fori_loop(0, n_chunks, body, 0)


def meridional(m, ky):
    ny, w, ch = m.shape
    taps = ky.shape[0]
    half = (taps - 1) // 2
    return pl.pallas_call(
        meridional_kernel,
        out_shape=jax.ShapeDtypeStruct(m.shape, BF16),
        in_specs=[VMEM_SPEC] * 2,
        out_specs=VMEM_SPEC,
        scratch_shapes=[pltpu.VMEM((ny + 2 * half, w, ch), F32)],
        compiler_params=SMALL_VMEM,
        cost_estimate=pl.CostEstimate(
            flops=2 * taps * m.size, transcendentals=0, bytes_accessed=4 * m.size
        ),
    )(m, ky)


def per_device(nt, increment, land_sea, kernel_x, kernel_y, balance):
    rows, nx, _ = increment.shape
    on_diagonal = lax.broadcasted_iota(jnp.int32, (rows, nx, nx), 1) == lax.broadcasted_iota(jnp.int32, (rows, nx, nx), 2)
    diag = lax.optimization_barrier(jnp.where(on_diagonal, land_sea[:, :, None], 0).astype(increment.dtype))
    masked = jnp.einsum("rxy,ryc->rxc", diag, increment, preferred_element_type=F32).astype(increment.dtype)
    z = zonal(masked, kernel_x)
    z_other = lax.ppermute(z, "comp", [(0, 1), (1, 0)])
    c = lax.axis_index("comp").astype(jnp.int32).reshape(1)
    mixed = balance_mix(c, z, z_other, balance, land_sea, nt)
    moved = lax.all_to_all(mixed, "tile", split_axis=0, concat_axis=0, tiled=True)
    nt_, rows, width, ch = moved.shape
    return meridional(moved.reshape(nt_ * rows, width, ch), kernel_y)


def solution(mesh):
    nt = mesh.shape["tile"]
    return jax.shard_map(
        functools.partial(per_device, nt),
        mesh=mesh,
        in_specs=(
            P(("ens", "tile"), None, "comp"),
            P("tile", None),
            P(None, "comp"),
            P(None, "comp"),
            P("tile", "comp", None),
        ),
        out_specs=P("ens", "tile", "comp"),
        check_vma=False,
    )
```

```python
import functools

import jax
import jax.numpy as jnp
from jax import lax
from jax.experimental import pallas as pl
from jax.experimental.pallas import tpu as pltpu
from jax.sharding import PartitionSpec as P

F32 = jnp.float32
VMEM_SPEC = pl.BlockSpec(memory_space=pltpu.VMEM)
SMALL_VMEM = pltpu.CompilerParams(vmem_limit_bytes=8 * 1024 * 1024)
BF16 = jnp.bfloat16


def zonal_kernel(m_ref, kx_ref, out_ref, ext_ref):
    rows, nx, ch = m_ref.shape
    taps = kx_ref.shape[0]
    half = (taps - 1) // 2
    pad = ((half + 7) // 8) * 8
    span = nx + 2 * pad - 8
    chunk = min(nx, 64)
    for r in range(rows):
        m = m_ref[r].astype(F32)
        ext = jnp.concatenate([m[nx - pad :], m, m[:pad]], axis=0)
        for s in range(8):
            ext_ref[s] = ext[s : s + span]

        def body(i, carry, r=r):
            x0 = pl.multiple_of(i * chunk, chunk)
            acc = jnp.zeros((chunk, ch), F32)
            for k in range(taps):
                e = k - half + pad
                q, s = divmod(e, 8)
                acc = acc + kx_ref[k : k + 1, :] * ext_ref[s, pl.ds(x0 + 8 * q, chunk), :]
            out_ref[r, pl.ds(x0, chunk), :] = acc.astype(out_ref.dtype)
            return carry

        n_chunks = nx // chunk
        lax.fori_loop(0, n_chunks, body, 0, unroll=n_chunks <= 4)


def zonal(m, kx):
    rows, nx, ch = m.shape
    taps = kx.shape[0]
    pad = (((taps - 1) // 2 + 7) // 8) * 8
    return pl.pallas_call(
        zonal_kernel,
        out_shape=jax.ShapeDtypeStruct(m.shape, BF16),
        in_specs=[VMEM_SPEC] * 2,
        out_specs=VMEM_SPEC,
        scratch_shapes=[pltpu.VMEM((8, nx + 2 * pad - 8, ch), F32)],
        compiler_params=SMALL_VMEM,
        cost_estimate=pl.CostEstimate(
            flops=2 * taps * m.size, transcendentals=0, bytes_accessed=4 * m.size
        ),
    )(m, kx)


def own_half_kernel(c_ref, z_ref, b_ref, out_ref):
    rows, _, ch = z_ref.shape
    c = c_ref[0]
    own = b_ref[0, :, pl.ds(pl.multiple_of(c * ch, ch), ch)]
    for r in range(rows):
        out_ref[r] = lax.dot_general(z_ref[r], own, (((1,), (1,)), ((), ())), preferred_element_type=F32)


def balance_kernel(c_ref, p_ref, zo_ref, b_ref, sea_ref, out_ref, seat_ref):
    nt, rows, width, _ = out_ref.shape
    nx, ch = zo_ref.shape[1], zo_ref.shape[2]
    sea = sea_ref[...].astype(F32)
    sea_pad = jnp.concatenate([sea, jnp.zeros((128 - rows, nx), F32)], axis=0)
    seat_ref[...] = jnp.transpose(sea_pad)
    c = c_ref[0]
    other = b_ref[0, :, pl.ds(pl.multiple_of((1 - c) * ch, ch), ch)]
    dims = (((1,), (1,)), ((), ()))
    for r in range(rows):
        res = p_ref[r] + lax.dot_general(zo_ref[r], other, dims, preferred_element_type=F32)
        res = (res * seat_ref[:, r : r + 1]).astype(out_ref.dtype)
        for t in range(nt):
            out_ref[t, r] = res[t * width : (t + 1) * width]


def balance_mix(c, z, zo, b, sea, nt):
    rows, nx, ch = z.shape
    ci = b.shape[1]
    smem = pl.BlockSpec(memory_space=pltpu.SMEM)
    partial = pl.pallas_call(
        own_half_kernel,
        out_shape=jax.ShapeDtypeStruct((rows, nx, ci), F32),
        in_specs=[smem] + [VMEM_SPEC] * 2,
        out_specs=VMEM_SPEC,
        compiler_params=SMALL_VMEM,
        cost_estimate=pl.CostEstimate(
            flops=2 * rows * nx * ch * ci,
            transcendentals=0,
            bytes_accessed=2 * (z.size + b.size) + 4 * rows * nx * ci,
        ),
    )(c, z, b)
    return pl.pallas_call(
        balance_kernel,
        out_shape=jax.ShapeDtypeStruct((nt, rows, nx // nt, ci), BF16),
        in_specs=[smem] + [VMEM_SPEC] * 4,
        out_specs=VMEM_SPEC,
        scratch_shapes=[pltpu.VMEM((nx, 128), F32)],
        compiler_params=SMALL_VMEM,
        cost_estimate=pl.CostEstimate(
            flops=2 * rows * nx * ch * ci,
            transcendentals=0,
            bytes_accessed=2 * (zo.size + b.size + rows * nx * ci) + 4 * rows * nx * ci,
        ),
    )(c, partial, zo, b, sea)


def meridional_kernel(m_ref, ky_ref, out_ref, pad_ref):
    ny, w, ch = m_ref.shape
    taps = ky_ref.shape[0]
    half = (taps - 1) // 2
    chunk = min(ny, 8)
    n_chunks = ny // chunk
    if n_chunks <= 8:
        pad_ref[0:ny] = m_ref[...].astype(F32)
        for c in range(n_chunks):
            y0 = c * chunk
            acc = [None] * chunk
            for k in range(taps):
                d = k - half
                lo, hi = max(0, -d - y0), min(chunk, ny - d - y0)
                if lo >= hi:
                    continue
                term = ky_ref[k : k + 1, :][None] * pad_ref[y0 + d + lo : y0 + d + hi]
                for y in range(lo, hi):
                    acc[y] = term[y - lo] if acc[y] is None else acc[y] + term[y - lo]
            out_ref[y0 : y0 + chunk] = jnp.stack(acc).astype(out_ref.dtype)
        return
    pad_ref[0:half] = jnp.zeros((half, w, ch), F32)
    pad_ref[half + ny :] = jnp.zeros((half, w, ch), F32)
    pad_ref[half : half + ny] = m_ref[...].astype(F32)

    def body(i, carry):
        y0 = pl.multiple_of(i * chunk, chunk)
        acc = jnp.zeros((chunk, w, ch), F32)
        for k in range(taps):
            acc = acc + ky_ref[k : k + 1, :][None] * pad_ref[pl.ds(y0 + k, chunk)]
        out_ref[pl.ds(y0, chunk)] = acc.astype(out_ref.dtype)
        return carry

    lax.fori_loop(0, n_chunks, body, 0)


def meridional(m, ky):
    ny, w, ch = m.shape
    taps = ky.shape[0]
    half = (taps - 1) // 2
    return pl.pallas_call(
        meridional_kernel,
        out_shape=jax.ShapeDtypeStruct(m.shape, BF16),
        in_specs=[VMEM_SPEC] * 2,
        out_specs=VMEM_SPEC,
        scratch_shapes=[pltpu.VMEM((ny + 2 * half, w, ch), F32)],
        compiler_params=SMALL_VMEM,
        cost_estimate=pl.CostEstimate(
            flops=2 * taps * m.size, transcendentals=0, bytes_accessed=4 * m.size
        ),
    )(m, ky)


def per_device(nt, increment, land_sea, kernel_x, kernel_y, balance):
    rows, nx, _ = increment.shape
    on_diagonal = lax.broadcasted_iota(jnp.int32, (rows, nx, nx), 1) == lax.broadcasted_iota(jnp.int32, (rows, nx, nx), 2)
    diag = lax.optimization_barrier(jnp.where(on_diagonal, land_sea[:, :, None], 0).astype(increment.dtype))
    masked = jnp.einsum("rxy,ryc->rxc", diag, increment, preferred_element_type=F32).astype(increment.dtype)
    z = zonal(masked, kernel_x)
    z_other = lax.ppermute(z, "comp", [(0, 1), (1, 0)])
    c = lax.axis_index("comp").astype(jnp.int32).reshape(1)
    mixed = balance_mix(c, z, z_other, balance, land_sea, nt)
    moved = lax.all_to_all(mixed, "tile", split_axis=0, concat_axis=0, tiled=True)
    nt_, rows, width, ch = moved.shape
    return meridional(moved.reshape(nt_ * rows, width, ch), kernel_y)


def solution(mesh):
    nt = mesh.shape["tile"]
    return jax.shard_map(
        functools.partial(per_device, nt),
        mesh=mesh,
        in_specs=(
            P(("ens", "tile"), None, "comp"),
            P("tile", None),
            P(None, "comp"),
            P(None, "comp"),
            P("tile", "comp", None),
        ),
        out_specs=P("ens", "tile", "comp"),
        check_vma=False,
    )
```

```python
import functools

import jax
import jax.numpy as jnp
from jax import lax
from jax.experimental import pallas as pl
from jax.experimental.pallas import tpu as pltpu
from jax.sharding import PartitionSpec as P

F32 = jnp.float32
VMEM_SPEC = pl.BlockSpec(memory_space=pltpu.VMEM)
SMALL_VMEM = pltpu.CompilerParams(vmem_limit_bytes=8 * 1024 * 1024)
BF16 = jnp.bfloat16


def zonal_kernel(m_ref, kx_ref, out_ref, ext_ref):
    rows, nx, ch = m_ref.shape
    taps = kx_ref.shape[0]
    half = (taps - 1) // 2
    pad = ((half + 7) // 8) * 8
    span = nx + 2 * pad - 8
    chunk = min(nx, 64)
    for r in range(rows):
        m = m_ref[r].astype(F32)
        ext = jnp.concatenate([m[nx - pad :], m, m[:pad]], axis=0)
        for s in range(8):
            ext_ref[s] = ext[s : s + span]

        def body(i, carry, r=r):
            x0 = pl.multiple_of(i * chunk, chunk)
            acc = jnp.zeros((chunk, ch), F32)
            for k in range(taps):
                e = k - half + pad
                q, s = divmod(e, 8)
                acc = acc + kx_ref[k : k + 1, :] * ext_ref[s, pl.ds(x0 + 8 * q, chunk), :]
            out_ref[r, pl.ds(x0, chunk), :] = acc.astype(out_ref.dtype)
            return carry

        n_chunks = nx // chunk
        lax.fori_loop(0, n_chunks, body, 0, unroll=n_chunks <= 4)


def zonal(m, kx):
    rows, nx, ch = m.shape
    taps = kx.shape[0]
    pad = (((taps - 1) // 2 + 7) // 8) * 8
    return pl.pallas_call(
        zonal_kernel,
        out_shape=jax.ShapeDtypeStruct(m.shape, BF16),
        in_specs=[VMEM_SPEC] * 2,
        out_specs=VMEM_SPEC,
        scratch_shapes=[pltpu.VMEM((8, nx + 2 * pad - 8, ch), F32)],
        compiler_params=SMALL_VMEM,
        cost_estimate=pl.CostEstimate(
            flops=2 * taps * m.size, transcendentals=0, bytes_accessed=4 * m.size
        ),
    )(m, kx)


def balance_kernel(c_ref, z_ref, zo_ref, b_ref, sea_ref, out_ref, seat_ref):
    nt, rows, width, _ = out_ref.shape
    nx, ch = z_ref.shape[1], z_ref.shape[2]
    sea = sea_ref[...].astype(F32)
    sea_pad = jnp.concatenate([sea, jnp.zeros((128 - rows, nx), F32)], axis=0)
    seat_ref[...] = jnp.transpose(sea_pad)
    c = c_ref[0]
    own = b_ref[0, :, pl.ds(pl.multiple_of(c * ch, ch), ch)]
    other = b_ref[0, :, pl.ds(pl.multiple_of((1 - c) * ch, ch), ch)]
    dims = (((1,), (1,)), ((), ()))
    for r in range(rows):
        res = lax.dot_general(z_ref[r], own, dims, preferred_element_type=F32)
        res = res + lax.dot_general(zo_ref[r], other, dims, preferred_element_type=F32)
        res = (res * seat_ref[:, r : r + 1]).astype(out_ref.dtype)
        for t in range(nt):
            out_ref[t, r] = res[t * width : (t + 1) * width]


def balance_mix(c, z, zo, b, sea, nt):
    rows, nx, ch = z.shape
    ci = b.shape[1]
    return pl.pallas_call(
        balance_kernel,
        out_shape=jax.ShapeDtypeStruct((nt, rows, nx // nt, ci), BF16),
        in_specs=[pl.BlockSpec(memory_space=pltpu.SMEM)] + [VMEM_SPEC] * 4,
        out_specs=VMEM_SPEC,
        scratch_shapes=[pltpu.VMEM((nx, 128), F32)],
        compiler_params=SMALL_VMEM,
        cost_estimate=pl.CostEstimate(
            flops=4 * rows * nx * ch * ci,
            transcendentals=0,
            bytes_accessed=2 * (2 * z.size + b.size + rows * nx * ci),
        ),
    )(c, z, zo, b, sea)


def meridional_kernel(m_ref, ky_ref, out_ref, pad_ref):
    ny, w, ch = m_ref.shape
    taps = ky_ref.shape[0]
    half = (taps - 1) // 2
    pad_ref[0:half] = jnp.zeros((half, w, ch), F32)
    pad_ref[half + ny :] = jnp.zeros((half, w, ch), F32)
    pad_ref[half : half + ny] = m_ref[...].astype(F32)
    chunk = min(ny, 2)
    n_chunks = ny // chunk

    def rows_at(y0, lo, hi):
        acc = jnp.zeros((chunk, w, ch), F32)
        for k in range(lo, hi):
            acc = acc + ky_ref[k : k + 1, :][None] * pad_ref[pl.ds(y0 + k, chunk)]
        out_ref[pl.ds(y0, chunk)] = acc.astype(out_ref.dtype)

    if n_chunks <= 16:
        for c in range(n_chunks):
            y0 = c * chunk
            lo = max(0, half - y0 - chunk + 1)
            hi = min(taps, half + ny - y0)
            rows_at(y0, lo, hi)
    else:

        def body(i, carry):
            rows_at(pl.multiple_of(i * chunk, chunk), 0, taps)
            return carry

        lax.fori_loop(0, n_chunks, body, 0)


def meridional(m, ky):
    ny, w, ch = m.shape
    taps = ky.shape[0]
    half = (taps - 1) // 2
    return pl.pallas_call(
        meridional_kernel,
        out_shape=jax.ShapeDtypeStruct(m.shape, BF16),
        in_specs=[VMEM_SPEC] * 2,
        out_specs=VMEM_SPEC,
        scratch_shapes=[pltpu.VMEM((ny + 2 * half, w, ch), F32)],
        compiler_params=SMALL_VMEM,
        cost_estimate=pl.CostEstimate(
            flops=2 * taps * m.size, transcendentals=0, bytes_accessed=4 * m.size
        ),
    )(m, ky)


def per_device(nt, increment, land_sea, kernel_x, kernel_y, balance):
    masked = increment * land_sea.astype(increment.dtype)[:, :, None]
    z = zonal(masked, kernel_x)
    z_other = lax.ppermute(z, "comp", [(0, 1), (1, 0)])
    c = lax.axis_index("comp").astype(jnp.int32).reshape(1)
    mixed = balance_mix(c, z, z_other, balance, land_sea, nt)
    moved = lax.all_to_all(mixed, "tile", split_axis=0, concat_axis=0, tiled=True)
    nt_, rows, width, ch = moved.shape
    return meridional(moved.reshape(nt_ * rows, width, ch), kernel_y)


def solution(mesh):
    nt = mesh.shape["tile"]
    return jax.shard_map(
        functools.partial(per_device, nt),
        mesh=mesh,
        in_specs=(
            P(("ens", "tile"), None, "comp"),
            P("tile", None),
            P(None, "comp"),
            P(None, "comp"),
            P("tile", "comp", None),
        ),
        out_specs=P("ens", "tile", "comp"),
        check_vma=False,
    )
```

```python
import functools

import jax
import jax.numpy as jnp
from jax import lax
from jax.experimental import pallas as pl
from jax.experimental.pallas import tpu as pltpu
from jax.sharding import PartitionSpec as P

F32 = jnp.float32
VMEM_SPEC = pl.BlockSpec(memory_space=pltpu.VMEM)
SMALL_VMEM = pltpu.CompilerParams(vmem_limit_bytes=8 * 1024 * 1024)
BF16 = jnp.bfloat16


def zonal_kernel(m_ref, kx_ref, out_ref, ext_ref):
    rows, nx, ch = m_ref.shape
    taps = kx_ref.shape[0]
    half = (taps - 1) // 2
    pad = ((half + 7) // 8) * 8
    span = nx + 2 * pad - 8
    chunk = min(nx, 64)
    for r in range(rows):
        m = m_ref[r].astype(F32)
        ext = jnp.concatenate([m[nx - pad :], m, m[:pad]], axis=0)
        for s in range(8):
            ext_ref[s] = ext[s : s + span]

        def body(i, carry, r=r):
            x0 = pl.multiple_of(i * chunk, chunk)
            acc = jnp.zeros((chunk, ch), F32)
            for k in range(taps):
                e = k - half + pad
                q, s = divmod(e, 8)
                acc = acc + kx_ref[k : k + 1, :] * ext_ref[s, pl.ds(x0 + 8 * q, chunk), :]
            out_ref[r, pl.ds(x0, chunk), :] = acc.astype(out_ref.dtype)
            return carry

        n_chunks = nx // chunk
        lax.fori_loop(0, n_chunks, body, 0, unroll=n_chunks <= 4)


def zonal(m, kx):
    rows, nx, ch = m.shape
    taps = kx.shape[0]
    pad = (((taps - 1) // 2 + 7) // 8) * 8
    return pl.pallas_call(
        zonal_kernel,
        out_shape=jax.ShapeDtypeStruct(m.shape, BF16),
        in_specs=[VMEM_SPEC] * 2,
        out_specs=VMEM_SPEC,
        scratch_shapes=[pltpu.VMEM((8, nx + 2 * pad - 8, ch), F32)],
        compiler_params=SMALL_VMEM,
        cost_estimate=pl.CostEstimate(
            flops=2 * taps * m.size, transcendentals=0, bytes_accessed=4 * m.size
        ),
    )(m, kx)


def own_half_kernel(c_ref, z_ref, b_ref, out_ref):
    rows, _, ch = z_ref.shape
    c = c_ref[0]
    own = b_ref[0, :, pl.ds(pl.multiple_of(c * ch, ch), ch)]
    for r in range(rows):
        out_ref[r] = lax.dot_general(z_ref[r], own, (((1,), (1,)), ((), ())), preferred_element_type=F32)


def balance_kernel(c_ref, p_ref, zo_ref, b_ref, sea_ref, out_ref, seat_ref):
    nt, rows, width, _ = out_ref.shape
    nx, ch = zo_ref.shape[1], zo_ref.shape[2]
    sea = sea_ref[...].astype(F32)
    sea_pad = jnp.concatenate([sea, jnp.zeros((128 - rows, nx), F32)], axis=0)
    seat_ref[...] = jnp.transpose(sea_pad)
    c = c_ref[0]
    other = b_ref[0, :, pl.ds(pl.multiple_of((1 - c) * ch, ch), ch)]
    dims = (((1,), (1,)), ((), ()))
    for r in range(rows):
        res = p_ref[r] + lax.dot_general(zo_ref[r], other, dims, preferred_element_type=F32)
        res = (res * seat_ref[:, r : r + 1]).astype(out_ref.dtype)
        for t in range(nt):
            out_ref[t, r] = res[t * width : (t + 1) * width]


def balance_mix(c, z, zo, b, sea, nt):
    rows, nx, ch = z.shape
    ci = b.shape[1]
    smem = pl.BlockSpec(memory_space=pltpu.SMEM)
    partial = pl.pallas_call(
        own_half_kernel,
        out_shape=jax.ShapeDtypeStruct((rows, nx, ci), F32),
        in_specs=[smem] + [VMEM_SPEC] * 2,
        out_specs=VMEM_SPEC,
        compiler_params=SMALL_VMEM,
        cost_estimate=pl.CostEstimate(
            flops=2 * rows * nx * ch * ci,
            transcendentals=0,
            bytes_accessed=2 * (z.size + b.size) + 4 * rows * nx * ci,
        ),
    )(c, z, b)
    return pl.pallas_call(
        balance_kernel,
        out_shape=jax.ShapeDtypeStruct((nt, rows, nx // nt, ci), BF16),
        in_specs=[smem] + [VMEM_SPEC] * 4,
        out_specs=VMEM_SPEC,
        scratch_shapes=[pltpu.VMEM((nx, 128), F32)],
        compiler_params=SMALL_VMEM,
        cost_estimate=pl.CostEstimate(
            flops=2 * rows * nx * ch * ci,
            transcendentals=0,
            bytes_accessed=2 * (zo.size + b.size + rows * nx * ci) + 4 * rows * nx * ci,
        ),
    )(c, partial, zo, b, sea)


def meridional_kernel(m_ref, ky_ref, out_ref, pad_ref):
    ny, w, ch = m_ref.shape
    taps = ky_ref.shape[0]
    half = (taps - 1) // 2
    pad_ref[0:half] = jnp.zeros((half, w, ch), F32)
    pad_ref[half + ny :] = jnp.zeros((half, w, ch), F32)
    pad_ref[half : half + ny] = m_ref[...].astype(F32)
    chunk = min(ny, 2)
    n_chunks = ny // chunk

    def rows_at(y0, lo, hi):
        acc = jnp.zeros((chunk, w, ch), F32)
        for k in range(lo, hi):
            acc = acc + ky_ref[k : k + 1, :][None] * pad_ref[pl.ds(y0 + k, chunk)]
        out_ref[pl.ds(y0, chunk)] = acc.astype(out_ref.dtype)

    if n_chunks <= 16:
        for c in range(n_chunks):
            y0 = c * chunk
            lo = max(0, half - y0 - chunk + 1)
            hi = min(taps, half + ny - y0)
            rows_at(y0, lo, hi)
    else:

        def body(i, carry):
            rows_at(pl.multiple_of(i * chunk, chunk), 0, taps)
            return carry

        lax.fori_loop(0, n_chunks, body, 0)


def meridional(m, ky):
    ny, w, ch = m.shape
    taps = ky.shape[0]
    half = (taps - 1) // 2
    return pl.pallas_call(
        meridional_kernel,
        out_shape=jax.ShapeDtypeStruct(m.shape, BF16),
        in_specs=[VMEM_SPEC] * 2,
        out_specs=VMEM_SPEC,
        scratch_shapes=[pltpu.VMEM((ny + 2 * half, w, ch), F32)],
        compiler_params=SMALL_VMEM,
        cost_estimate=pl.CostEstimate(
            flops=2 * taps * m.size, transcendentals=0, bytes_accessed=4 * m.size
        ),
    )(m, ky)


def per_device(nt, increment, land_sea, kernel_x, kernel_y, balance):
    rows, nx, _ = increment.shape
    on_diagonal = lax.broadcasted_iota(jnp.int32, (rows, nx, nx), 1) == lax.broadcasted_iota(jnp.int32, (rows, nx, nx), 2)
    diag = lax.optimization_barrier(jnp.where(on_diagonal, land_sea[:, :, None], 0).astype(increment.dtype))
    masked = jnp.einsum("rxy,ryc->rxc", diag, increment, preferred_element_type=F32).astype(increment.dtype)
    z = zonal(masked, kernel_x)
    z_other = lax.ppermute(z, "comp", [(0, 1), (1, 0)])
    c = lax.axis_index("comp").astype(jnp.int32).reshape(1)
    mixed = balance_mix(c, z, z_other, balance, land_sea, nt)
    moved = lax.all_to_all(mixed, "tile", split_axis=0, concat_axis=0, tiled=True)
    nt_, rows, width, ch = moved.shape
    return meridional(moved.reshape(nt_ * rows, width, ch), kernel_y)


def solution(mesh):
    nt = mesh.shape["tile"]
    return jax.shard_map(
        functools.partial(per_device, nt),
        mesh=mesh,
        in_specs=(
            P(("ens", "tile"), None, "comp"),
            P("tile", None),
            P(None, "comp"),
            P(None, "comp"),
            P("tile", "comp", None),
        ),
        out_specs=P("ens", "tile", "comp"),
        check_vma=False,
    )
```
